256 devices in a mesh: bond: 64 (over z, y, core), mpo: 4 (over x).
Axes of the slice: x: 4, y: 4, z: 8, core: 2. Of those that a mesh axis runs over, the one named last changes fastest.
Arguments:
- wave_blocks: bfloat16 [256, 8, 64, 256], P('bond'), may hold values from -6 to 6
- left_env: bfloat16 [256, 20, 4096], P('bond', 'mpo'), may hold values from -0.75 to 0.75
- right_env: bfloat16 [256, 20, 4096], P('bond', 'mpo'), may hold values from -0.75 to 0.75
- mpo_coef: float32 [20, 8], P('mpo'), may hold values from -3 to 3
- mpo_mask: int32 [20, 8], P('mpo'), may hold values 0 or 1
- right_sector: int32 [256, 8], replicated, may hold values from 0 to 255, as said below
Outputs:
- sigma_blocks: bfloat16 [256, 8, 64, 256], P('bond')
The draws below stay inside these ranges and needn't reach their ends.
Inputs may be any that keep to these rules, and one draw needn't show every extreme that they name: `right_sector`: right sector b is held by bond device b // 4. The 32 blocks of the left sectors of one bond device (rows in order) name sectors of at most 1 block on any one bond device, and exactly 1 on some.
All inputs are finite; a program needn't handle non-finite values. No bound on the sum of `mpo_mask` on one device may be relied on, other than what follows from the above.
Results may differ from the reference program's by a relative error of at most 0.013.
Values may be sent and summed in bfloat16 or wider, within the bound.
No kernel may reach another device: no remote copies, remote signals or barrier semaphores. Data moves between devices by JAX's collectives and lax.ppermute only.
A program may use at most 128 MiB of HBM per device.

```python
import jax
import jax.numpy as jnp
from jax import lax

BLK = 64
NSEC = 256
NPB = 8
TERMS = 20
NVEC = 4
SEC_DEV = 4
NB_DEV = 32
CAP = 1
N_BOND = 64
N_MPO = 4


def draw_right_sector(key, part):
    key_list = jax.random.split(key, 5)
    slot_total = N_BOND * CAP
    slot_owner = jnp.arange(slot_total, dtype=jnp.int32) // CAP
    busy_level = jax.random.randint(key_list[0], (N_BOND,), 0, 4)
    favorite = jax.random.randint(key_list[1], (N_BOND,), 0, N_BOND)
    noise_part = jax.random.randint(key_list[2], (N_BOND, slot_total), 0, 4096)
    scores = noise_part + busy_level[slot_owner][None, :] * 4096
    scores = scores + (slot_owner[None, :] == favorite[:, None]).astype(jnp.int32) * 65536
    scores = scores * slot_total + jnp.arange(slot_total, dtype=jnp.int32)[None, :]
    chosen = lax.top_k(scores, NB_DEV)[1].astype(jnp.int32)
    shuffle_keys = jax.random.randint(key_list[3], (N_BOND, NB_DEV), 0, 1 << 20) * NB_DEV
    shuffle_keys = shuffle_keys + jnp.arange(NB_DEV, dtype=jnp.int32)[None, :]
    order_ids = jnp.argsort(shuffle_keys, axis=1)
    chosen = jnp.take_along_axis(chosen, order_ids, axis=1)
    local_ids = jax.random.randint(key_list[4], (N_BOND, NB_DEV), 0, SEC_DEV)
    return (chosen // CAP * SEC_DEV + local_ids).reshape(NSEC, NPB).astype(jnp.int32)


def plant(values, rng, smallest, top_value):
    spot = [jax.random.randint(jax.random.fold_in(rng, axis), (), 0, length) for axis, length in enumerate(values.shape)]
    main_axis = values.shape.index(max(values.shape))
    beside = spot[:main_axis] + [(spot[main_axis] + 1) % values.shape[main_axis]] + spot[main_axis + 1:]
    return values.at[tuple(spot)].set(smallest).at[tuple(beside)].set(top_value)


def shard_levels(rng, shape, cuts, low, high):
    loudness = 1.0
    for axis_at, parts in cuts:
        steps = jax.random.uniform(jax.random.fold_in(jax.random.fold_in(rng, 6), axis_at), (parts,), jnp.float32, low / len(cuts), high / len(cuts))
        loudness = loudness * jnp.repeat(jnp.exp(steps), shape[axis_at] // parts).reshape((-1,) + (1,) * (len(shape) - 1 - axis_at))
    return loudness


def normal_values(own_key, extent, width, limit, cuts=(), kind=jnp.bfloat16):
    values = jax.random.normal(own_key, extent, jnp.float32) * width
    if len(cuts) > 0:
        values = shard_levels(own_key, extent, cuts, -0.22, 0.18) * values
    return jnp.clip(values, min=-limit, max=limit).astype(kind)


def setup_inputs(seed: int = 0) -> dict:
    seeds = jax.random.split(jax.random.key(seed), 7)
    wave_blocks = normal_values(seeds[0], (NSEC, NPB, BLK, NVEC * BLK), 1.0, 6.0, ((0, 64),))
    left_env = normal_values(seeds[1], (NSEC, TERMS, BLK * BLK), BLK ** -0.5, 0.75, ((0, 64), (1, 4)))
    right_env = normal_values(seeds[2], (NSEC, TERMS, BLK * BLK), BLK ** -0.5, 0.75, ((0, 64), (1, 4)))
    mpo_coef = normal_values(seeds[3], (TERMS, NPB), 0.5, 3.0, ((0, 4),), jnp.float32)
    mpo_mask = plant((jax.random.randint(seeds[4], (TERMS, NPB), 0, 2) < 1).astype(jnp.int32), jax.random.fold_in(seeds[4], 1), 0, 1)
    right_sector = draw_right_sector(jax.random.fold_in(seeds[6], 71), 0)
    return {"wave_blocks": wave_blocks, "left_env": left_env, "right_env": right_env, "mpo_coef": mpo_coef, "mpo_mask": mpo_mask, "right_sector": right_sector}


def to_bfloat(values):
    return lax.optimization_barrier(values.astype(jnp.bfloat16)).astype(jnp.float32)


def reference(wave_blocks, left_env, right_env, mpo_coef, mpo_mask, right_sector):
    term_gains = mpo_coef * mpo_mask.astype(jnp.float32)
    group_terms = TERMS // N_MPO

    def per_sector(sector_id):
        wave_local = wave_blocks[sector_id].astype(jnp.float32)
        left_local = left_env[sector_id].astype(jnp.float32).reshape(TERMS, BLK, BLK)
        left_scaled = to_bfloat(term_gains[:, :, None, None] * left_local[:, None, :, :])
        sectioned = to_bfloat(jnp.einsum("wjlk,jkc->wjlc", left_scaled, wave_local))
        sectioned = sectioned.reshape(N_MPO, group_terms, NPB, BLK, NVEC, BLK)
        right_ids = right_sector[sector_id].astype(jnp.int32)
        right_local = right_env[right_ids].astype(jnp.float32).reshape(NPB, N_MPO, group_terms, BLK, BLK)
        group_part = to_bfloat(jnp.einsum("mtjlvr,jmtsr->mjlvs", sectioned, right_local))
        summed = jnp.sum(group_part, axis=0)
        return summed.astype(jnp.bfloat16).reshape(NPB, BLK, NVEC * BLK)

    return lax.map(per_sector, jnp.arange(NSEC, dtype=jnp.int32))
```

```python
import jax
import jax.numpy as jnp
from jax import lax
from jax.experimental import pallas as pl
from jax.experimental.pallas import tpu as pltpu
from jax.sharding import PartitionSpec as P


def block_kernel(gain_ref, wave_ref, left_ref, right_ref, out_ref):
    block_count, block_width, column_count = wave_ref.shape
    classes = gain_ref.shape[1]
    term_count = gain_ref.shape[0]
    rows = term_count * block_width
    vectors = column_count // block_width
    tile_rows = lax.broadcasted_iota(jnp.int32, (block_width, column_count), 0)
    tile_cols = lax.broadcasted_iota(jnp.int32, (block_width, column_count), 1)
    lane_tile = (tile_rows == tile_cols % block_width).astype(jnp.bfloat16)
    diag_rows = lax.broadcasted_iota(jnp.int32, (column_count, column_count), 0)
    diag_cols = lax.broadcasted_iota(jnp.int32, (column_count, column_count), 1)
    diagonal = diag_rows // block_width == diag_cols // block_width

    def body(b, carry):
        sector = b // classes
        charge = b % classes
        wave = wave_ref[b]
        scaled = []
        for w in range(term_count):
            piece = left_ref[sector, w * block_width:(w + 1) * block_width, :]
            scaled.append(
                (piece.astype(jnp.float32) * gain_ref[w, charge]).astype(jnp.bfloat16)
            )
        left_scaled = jnp.concatenate(scaled, axis=0)
        sectioned = jnp.dot(
            left_scaled, wave, preferred_element_type=jnp.float32
        ).astype(jnp.bfloat16)
        tiled = jnp.dot(
            right_ref[b], lane_tile, preferred_element_type=jnp.float32
        ).astype(jnp.bfloat16)
        acc = jnp.zeros((block_width, column_count), jnp.float32)
        for w in range(term_count):
            part = tiled[w * block_width:(w + 1) * block_width]
            expanded = jnp.concatenate([part] * vectors, axis=0)
            expanded = jnp.where(diagonal, expanded, jnp.zeros_like(expanded))
            acc = acc + jnp.dot(
                sectioned[w * block_width:(w + 1) * block_width],
                expanded,
                preferred_element_type=jnp.float32,
            )
        out_ref[b] = acc.astype(out_ref.dtype)
        return carry

    lax.fori_loop(0, block_count, body, 0)


def apply_blocks(gains, wave_rows, left_rows, right_rows):
    block_count, block_width, column_count = wave_rows.shape
    rows = right_rows.shape[1]
    flops = block_count * (
        2 * 2 * rows * block_width * column_count
        + 2 * rows * column_count * column_count
    )
    bytes_accessed = 2 * (
        2 * wave_rows.size + left_rows.size + right_rows.size
    )
    vmem = pltpu.MemorySpace.VMEM if hasattr(pltpu, "MemorySpace") else pltpu.VMEM
    return pl.pallas_call(
        block_kernel,
        out_shape=jax.ShapeDtypeStruct(wave_rows.shape, jnp.bfloat16),
        in_specs=[
            pl.BlockSpec(memory_space=pltpu.SMEM),
            pl.BlockSpec(memory_space=vmem),
            pl.BlockSpec(memory_space=vmem),
            pl.BlockSpec(memory_space=vmem),
        ],
        out_specs=pl.BlockSpec(memory_space=vmem),
        cost_estimate=pl.CostEstimate(
            flops=flops, bytes_accessed=bytes_accessed, transcendentals=0
        ),
    )(gains, wave_rows, left_rows, right_rows)


def per_device(wave_blocks, left_env, right_env, mpo_coef, mpo_mask, right_sector):
    sec_local, class_count, block_width, column_count = wave_blocks.shape
    term_local = left_env.shape[1]
    blocks_local = sec_local * class_count
    bond_count = lax.axis_size("bond")
    bond_index = lax.axis_index("bond")
    gains = mpo_coef * mpo_mask.astype(jnp.float32)

    requests = right_sector.reshape(bond_count, blocks_local)
    hits = (requests // sec_local) == bond_index
    send_sector = jnp.sum(
        jnp.where(hits, requests % sec_local, 0), axis=1
    ).astype(jnp.int32)
    right_t = jnp.swapaxes(
        right_env.reshape(sec_local, term_local, block_width, block_width), 2, 3
    ).reshape(sec_local, term_local, block_width * block_width)
    send_right = jnp.take(right_t, send_sector, axis=0)
    got_right = lax.all_to_all(send_right, "bond", split_axis=0, concat_axis=0, tiled=True)

    mine = lax.dynamic_slice_in_dim(requests, bond_index, 1, axis=0).reshape(blocks_local)
    right_rows = jnp.take(got_right, mine // sec_local, axis=0).reshape(
        blocks_local, term_local * block_width, block_width
    )
    left_rows = left_env.reshape(sec_local, term_local * block_width, block_width)
    wave_rows = wave_blocks.reshape(blocks_local, block_width, column_count)
    partial_sum = apply_blocks(gains, wave_rows, left_rows, right_rows)
    summed = lax.psum(partial_sum, "mpo")
    return summed.reshape(wave_blocks.shape)


def solution(mesh):
    return jax.shard_map(
        per_device,
        mesh=mesh,
        in_specs=(
            P("bond", None, None, None),
            P("bond", "mpo", None),
            P("bond", "mpo", None),
            P("mpo", None),
            P("mpo", None),
            P(),
        ),
        out_specs=P("bond", None, None, None),
        check_vma=False,
    )
```

```python
import jax
import jax.numpy as jnp
from jax import lax
from jax.experimental import pallas as pl
from jax.experimental.pallas import tpu as pltpu
from jax.sharding import PartitionSpec as P


def block_kernel(gain_ref, source_ref, wave_ref, left_ref, right_ref, out_ref):
    block_count, block_width, column_count = wave_ref.shape
    classes = gain_ref.shape[1]
    term_count = gain_ref.shape[0]
    rows = term_count * block_width
    vectors = column_count // block_width
    lanes = right_ref.shape[2]
    half_rows = block_width // 2
    tile_rows = lax.broadcasted_iota(jnp.int32, (lanes, 2 * column_count), 0)
    tile_cols = lax.broadcasted_iota(jnp.int32, (lanes, 2 * column_count), 1)
    lane_tile = (
        (tile_rows // block_width == tile_cols // column_count)
        & (tile_rows % block_width == tile_cols % block_width)
    ).astype(jnp.bfloat16)
    diag_rows = lax.broadcasted_iota(jnp.int32, (column_count, column_count), 0)
    diag_cols = lax.broadcasted_iota(jnp.int32, (column_count, column_count), 1)
    diagonal = diag_rows // block_width == diag_cols // block_width

    def body(b, carry):
        sector = b // classes
        charge = b % classes
        wave = wave_ref[b]
        scaled = []
        for w in range(term_count):
            piece = left_ref[sector, w * block_width:(w + 1) * block_width, :]
            scaled.append(
                (piece.astype(jnp.float32) * gain_ref[w, charge]).astype(jnp.bfloat16)
            )
        left_scaled = jnp.concatenate(scaled, axis=0)
        sectioned = jnp.dot(
            left_scaled, wave, preferred_element_type=jnp.float32
        ).astype(jnp.bfloat16)
        tiled = jnp.dot(
            right_ref[source_ref[b]], lane_tile, preferred_element_type=jnp.float32
        ).astype(jnp.bfloat16)
        acc = jnp.zeros((block_width, column_count), jnp.float32)
        for w in range(term_count):
            rows_w = tiled[w * half_rows:(w + 1) * half_rows]
            part = jnp.concatenate(
                [rows_w[:, :column_count], rows_w[:, column_count:]], axis=0
            )
            expanded = jnp.concatenate([part] * vectors, axis=0)
            expanded = jnp.where(diagonal, expanded, jnp.zeros_like(expanded))
            acc = acc + jnp.dot(
                sectioned[w * block_width:(w + 1) * block_width],
                expanded,
                preferred_element_type=jnp.float32,
            )
        out_ref[b] = acc.astype(out_ref.dtype)
        return carry

    lax.fori_loop(0, block_count, body, 0)


def apply_blocks(gains, sources, wave_rows, left_rows, right_rows):
    block_count, block_width, column_count = wave_rows.shape
    rows = left_rows.shape[1]
    flops = block_count * (
        2 * 2 * rows * block_width * column_count
        + 2 * rows * column_count * column_count
    )
    bytes_accessed = 2 * (
        2 * wave_rows.size + left_rows.size + right_rows.size
    )
    vmem = pltpu.MemorySpace.VMEM if hasattr(pltpu, "MemorySpace") else pltpu.VMEM
    return pl.pallas_call(
        block_kernel,
        out_shape=jax.ShapeDtypeStruct(wave_rows.shape, jnp.bfloat16),
        in_specs=[
            pl.BlockSpec(memory_space=pltpu.SMEM),
            pl.BlockSpec(memory_space=pltpu.SMEM),
            pl.BlockSpec(memory_space=vmem),
            pl.BlockSpec(memory_space=vmem),
            pl.BlockSpec(memory_space=vmem),
        ],
        out_specs=pl.BlockSpec(memory_space=vmem),
        cost_estimate=pl.CostEstimate(
            flops=flops, bytes_accessed=bytes_accessed, transcendentals=0
        ),
    )(gains, sources, wave_rows, left_rows, right_rows)


def per_device(wave_blocks, left_env, right_env, mpo_coef, mpo_mask, right_sector):
    sec_local, class_count, block_width, column_count = wave_blocks.shape
    term_local = left_env.shape[1]
    blocks_local = sec_local * class_count
    bond_count = lax.axis_size("bond")
    bond_index = lax.axis_index("bond")
    gains = mpo_coef * mpo_mask.astype(jnp.float32)

    requests = right_sector.reshape(bond_count, blocks_local)
    hits = (requests // sec_local) == bond_index
    send_sector = jnp.sum(
        jnp.where(hits, requests % sec_local, 0), axis=1
    ).astype(jnp.int32)
    half_rows = block_width // 2
    right_t = jnp.transpose(
        right_env.reshape(sec_local, term_local, block_width, 2, half_rows),
        (0, 1, 4, 3, 2),
    ).reshape(sec_local, term_local * half_rows, 2 * block_width)
    send_right = jnp.take(right_t, send_sector, axis=0, mode="clip")
    got_right = lax.all_to_all(send_right, "bond", split_axis=0, concat_axis=0, tiled=True)

    mine = lax.dynamic_slice_in_dim(requests, bond_index, 1, axis=0).reshape(blocks_local)
    sources = (mine // sec_local).astype(jnp.int32)
    left_rows = left_env.reshape(sec_local, term_local * block_width, block_width)
    wave_rows = wave_blocks.reshape(blocks_local, block_width, column_count)
    partial_sum = apply_blocks(gains, sources, wave_rows, left_rows, got_right)
    summed = lax.psum(partial_sum, "mpo")
    return summed.reshape(wave_blocks.shape)


def solution(mesh):
    return jax.shard_map(
        per_device,
        mesh=mesh,
        in_specs=(
            P("bond", None, None, None),
            P("bond", "mpo", None),
            P("bond", "mpo", None),
            P("mpo", None),
            P("mpo", None),
            P(),
        ),
        out_specs=P("bond", None, None, None),
        check_vma=False,
    )
```

```python
import jax
import jax.numpy as jnp
from jax import lax
from jax.experimental import pallas as pl
from jax.experimental.pallas import tpu as pltpu
from jax.sharding import PartitionSpec as P


def block_kernel(gain_ref, source_ref, wave_ref, left_ref, right_ref, out_ref):
    block_count, block_width, column_count = wave_ref.shape
    classes = gain_ref.shape[1]
    term_count = gain_ref.shape[0]
    rows = term_count * block_width
    vectors = column_count // block_width
    lanes = right_ref.shape[2]
    half_rows = block_width // 2
    tile_rows = lax.broadcasted_iota(jnp.int32, (lanes, 2 * column_count), 0)
    tile_cols = lax.broadcasted_iota(jnp.int32, (lanes, 2 * column_count), 1)
    lane_tile = (
        (tile_rows // block_width == tile_cols // column_count)
        & (tile_rows % block_width == tile_cols % block_width)
    ).astype(jnp.bfloat16)
    diag_rows = lax.broadcasted_iota(jnp.int32, (column_count, column_count), 0)
    diag_cols = lax.broadcasted_iota(jnp.int32, (column_count, column_count), 1)
    diagonal = diag_rows // block_width == diag_cols // block_width

    def body(b, carry):
        sector = b // classes
        charge = b % classes
        wave = wave_ref[b]
        scaled = []
        for w in range(term_count):
            piece = left_ref[sector, w * block_width:(w + 1) * block_width, :]
            scaled.append(
                (piece.astype(jnp.float32) * gain_ref[w, charge]).astype(jnp.bfloat16)
            )
        left_scaled = jnp.concatenate(scaled, axis=0)
        sectioned = jnp.dot(
            left_scaled, wave, preferred_element_type=jnp.float32
        ).astype(jnp.bfloat16)
        tiled = jnp.dot(
            right_ref[source_ref[b]], lane_tile, preferred_element_type=jnp.float32
        ).astype(jnp.bfloat16)
        acc = jnp.zeros((block_width, column_count), jnp.float32)
        for w in range(term_count):
            rows_w = tiled[w * half_rows:(w + 1) * half_rows]
            part = jnp.concatenate(
                [rows_w[:, :column_count], rows_w[:, column_count:]], axis=0
            )
            expanded = jnp.concatenate([part] * vectors, axis=0)
            expanded = jnp.where(diagonal, expanded, jnp.zeros_like(expanded))
            acc = acc + jnp.dot(
                sectioned[w * block_width:(w + 1) * block_width],
                expanded,
                preferred_element_type=jnp.float32,
            )
        out_ref[b] = acc.astype(out_ref.dtype)
        return carry

    lax.fori_loop(0, block_count, body, 0)


def apply_blocks(gains, sources, wave_rows, left_rows, right_rows):
    block_count, block_width, column_count = wave_rows.shape
    rows = left_rows.shape[1]
    flops = block_count * (
        2 * 2 * rows * block_width * column_count
        + 2 * rows * column_count * column_count
    )
    bytes_accessed = 2 * (
        2 * wave_rows.size + left_rows.size + right_rows.size
    )
    vmem = pltpu.MemorySpace.VMEM if hasattr(pltpu, "MemorySpace") else pltpu.VMEM
    return pl.pallas_call(
        block_kernel,
        out_shape=jax.ShapeDtypeStruct(wave_rows.shape, jnp.bfloat16),
        in_specs=[
            pl.BlockSpec(memory_space=pltpu.SMEM),
            pl.BlockSpec(memory_space=pltpu.SMEM),
            pl.BlockSpec(memory_space=vmem),
            pl.BlockSpec(memory_space=vmem),
            pl.BlockSpec(memory_space=vmem),
        ],
        out_specs=pl.BlockSpec(memory_space=vmem),
        cost_estimate=pl.CostEstimate(
            flops=flops, bytes_accessed=bytes_accessed, transcendentals=0
        ),
    )(gains, sources, wave_rows, left_rows, right_rows)


def per_device(wave_blocks, left_env, right_env, mpo_coef, mpo_mask, right_sector):
    sec_local, class_count, block_width, column_count = wave_blocks.shape
    term_local = left_env.shape[1]
    blocks_local = sec_local * class_count
    bond_count = lax.axis_size("bond")
    bond_index = lax.axis_index("bond")
    gains = mpo_coef * mpo_mask.astype(jnp.float32)

    requests = right_sector.reshape(bond_count, blocks_local)
    hits = (requests // sec_local) == bond_index
    send_sector = jnp.sum(
        jnp.where(hits, requests % sec_local, 0), axis=1
    ).astype(jnp.int32)
    half_rows = block_width // 2
    right_t = jnp.transpose(
        right_env.reshape(sec_local, term_local, block_width, 2, half_rows),
        (0, 1, 4, 3, 2),
    ).reshape(sec_local, term_local * half_rows, 2 * block_width)
    send_right = jnp.take(right_t, send_sector, axis=0, mode="clip")
    got_right = lax.all_to_all(send_right, "bond", split_axis=0, concat_axis=0, tiled=True)

    mine = lax.dynamic_slice_in_dim(requests, bond_index, 1, axis=0).reshape(blocks_local)
    sources = (mine // sec_local).astype(jnp.int32)
    left_rows = left_env.reshape(sec_local, term_local * block_width, block_width)
    wave_rows = wave_blocks.reshape(blocks_local, block_width, column_count)
    partial_sum = apply_blocks(gains, sources, wave_rows, left_rows, got_right)
    mpo_count = lax.axis_size("mpo")
    mpo_index = lax.axis_index("mpo")
    parts = [partial_sum]
    for shift in range(1, mpo_count):
        pairs = [(i, (i + shift) % mpo_count) for i in range(mpo_count)]
        parts.append(lax.ppermute(partial_sum, "mpo", pairs))
    stacked = jnp.stack(parts)
    summed = jnp.zeros(partial_sum.shape, jnp.float32)
    for group in range(mpo_count):
        at = (mpo_index - group) % mpo_count
        summed = summed + lax.dynamic_index_in_dim(
            stacked, at, 0, keepdims=False
        ).astype(jnp.float32)
    return summed.astype(jnp.bfloat16).reshape(wave_blocks.shape)


def solution(mesh):
    return jax.shard_map(
        per_device,
        mesh=mesh,
        in_specs=(
            P("bond", None, None, None),
            P("bond", "mpo", None),
            P("bond", "mpo", None),
            P("mpo", None),
            P("mpo", None),
            P(),
        ),
        out_specs=P("bond", None, None, None),
        check_vma=False,
    )
```

```python
import jax
import jax.numpy as jnp
from jax import lax
from jax.experimental import pallas as pl
from jax.experimental.pallas import tpu as pltpu
from jax.sharding import PartitionSpec as P


def block_kernel(gain_ref, wave_ref, left_ref, right_ref, out_ref):
    block_count, block_width, column_count = wave_ref.shape
    group_count = left_ref.shape[0]
    term_count = gain_ref.shape[0] // group_count
    vectors = column_count // block_width
    lanes = right_ref.shape[3]
    half_rows = block_width // 2
    tile_rows = lax.broadcasted_iota(jnp.int32, (lanes, 2 * column_count), 0)
    tile_cols = lax.broadcasted_iota(jnp.int32, (lanes, 2 * column_count), 1)
    lane_tile = (
        (tile_rows // block_width == tile_cols // column_count)
        & (tile_rows % block_width == tile_cols % block_width)
    ).astype(jnp.bfloat16)
    diag_rows = lax.broadcasted_iota(jnp.int32, (column_count, column_count), 0)
    diag_cols = lax.broadcasted_iota(jnp.int32, (column_count, column_count), 1)
    diagonal = diag_rows // block_width == diag_cols // block_width

    def body(b, carry):
        wave = wave_ref[b]
        total = jnp.zeros((block_width, column_count), jnp.float32)
        for g in range(group_count):
            scaled = []
            for w in range(term_count):
                piece = left_ref[g, w * block_width:(w + 1) * block_width, :]
                gain = gain_ref[g * term_count + w, b]
                scaled.append((piece.astype(jnp.float32) * gain).astype(jnp.bfloat16))
            left_scaled = jnp.concatenate(scaled, axis=0)
            sectioned = jnp.dot(
                left_scaled, wave, preferred_element_type=jnp.float32
            ).astype(jnp.bfloat16)
            tiled = jnp.dot(
                right_ref[g, b], lane_tile, preferred_element_type=jnp.float32
            ).astype(jnp.bfloat16)
            acc = jnp.zeros((block_width, column_count), jnp.float32)
            for w in range(term_count):
                rows_w = tiled[w * half_rows:(w + 1) * half_rows]
                part = jnp.concatenate(
                    [rows_w[:, :column_count], rows_w[:, column_count:]], axis=0
                )
                expanded = jnp.concatenate([part] * vectors, axis=0)
                expanded = jnp.where(diagonal, expanded, jnp.zeros_like(expanded))
                acc = acc + jnp.dot(
                    sectioned[w * block_width:(w + 1) * block_width],
                    expanded,
                    preferred_element_type=jnp.float32,
                )
            total = total + acc.astype(jnp.bfloat16).astype(jnp.float32)
        out_ref[b] = total.astype(out_ref.dtype)
        return carry

    lax.fori_loop(0, block_count, body, 0)


def apply_blocks(gains, wave_rows, left_rows, right_rows):
    block_count, block_width, column_count = wave_rows.shape
    group_count, rows = left_rows.shape[0], left_rows.shape[1]
    flops = block_count * group_count * (
        2 * 2 * rows * block_width * column_count
        + 2 * rows * column_count * column_count
    )
    bytes_accessed = 2 * (
        2 * wave_rows.size + left_rows.size + right_rows.size
    )
    vmem = pltpu.MemorySpace.VMEM if hasattr(pltpu, "MemorySpace") else pltpu.VMEM
    return pl.pallas_call(
        block_kernel,
        out_shape=jax.ShapeDtypeStruct(wave_rows.shape, jnp.bfloat16),
        in_specs=[
            pl.BlockSpec(memory_space=pltpu.SMEM),
            pl.BlockSpec(memory_space=vmem),
            pl.BlockSpec(memory_space=vmem),
            pl.BlockSpec(memory_space=vmem),
        ],
        out_specs=pl.BlockSpec(memory_space=vmem),
        cost_estimate=pl.CostEstimate(
            flops=flops, bytes_accessed=bytes_accessed, transcendentals=0
        ),
    )(gains, wave_rows, left_rows, right_rows)


def shifted(value, shift, count):
    pairs = [(i, (i + shift) % count) for i in range(count)]
    return lax.ppermute(value, "mpo", pairs)


def per_device(wave_blocks, left_env, right_env, mpo_coef, mpo_mask, right_sector):
    sec_local, class_count, block_width, column_count = wave_blocks.shape
    term_local = left_env.shape[1]
    blocks_local = sec_local * class_count
    bond_count = lax.axis_size("bond")
    bond_index = lax.axis_index("bond")
    mpo_count = lax.axis_size("mpo")
    mpo_index = lax.axis_index("mpo")
    half_rows = block_width // 2
    gains = mpo_coef * mpo_mask.astype(jnp.float32)

    requests = right_sector.reshape(bond_count, blocks_local)
    hits = (requests // sec_local) == bond_index
    send_sector = jnp.sum(
        jnp.where(hits, requests % sec_local, 0), axis=1
    ).astype(jnp.int32)
    right_t = jnp.transpose(
        right_env.reshape(sec_local, term_local, block_width, 2, half_rows),
        (0, 1, 4, 3, 2),
    ).reshape(sec_local, term_local * half_rows, 2 * block_width)
    send_right = jnp.take(right_t, send_sector, axis=0, mode="clip")
    got_right = lax.all_to_all(send_right, "bond", split_axis=0, concat_axis=0, tiled=True)

    left_flat = left_env.reshape(sec_local, term_local * half_rows, 2 * block_width)
    left_parts = [lax.dynamic_index_in_dim(left_flat, mpo_index, 0, keepdims=False)]
    gain_parts = [gains]
    for shift in range(1, mpo_count):
        target = (mpo_index + shift) % mpo_count
        left_parts.append(
            shifted(lax.dynamic_index_in_dim(left_flat, target, 0, keepdims=False), shift, mpo_count)
        )
        gain_parts.append(shifted(gains, shift, mpo_count))
    left_rows = jnp.stack(left_parts).reshape(
        mpo_count, term_local * block_width, block_width
    )
    gain_rows = jnp.stack(gain_parts).reshape(mpo_count * term_local, class_count)

    mine = lax.dynamic_slice_in_dim(requests, bond_index, 1, axis=0).reshape(
        sec_local, class_count
    )
    sources = (mine // sec_local).astype(jnp.int32)
    right_parts = []
    for shift in range(mpo_count):
        target = (mpo_index + shift) % mpo_count
        picked = jnp.take(
            got_right,
            lax.dynamic_index_in_dim(sources, target, 0, keepdims=False),
            axis=0,
            mode="clip",
        )
        right_parts.append(picked if shift == 0 else shifted(picked, shift, mpo_count))
    right_rows = jnp.stack(right_parts)

    wave_rows = lax.dynamic_index_in_dim(wave_blocks, mpo_index, 0, keepdims=False)
    done = apply_blocks(gain_rows, wave_rows, left_rows, right_rows)

    out_parts = [done] + [shifted(done, shift, mpo_count) for shift in range(1, mpo_count)]
    stacked = jnp.stack(out_parts)
    order = (mpo_index - jnp.arange(mpo_count, dtype=jnp.int32)) % mpo_count
    return jnp.take(stacked, order, axis=0, mode="clip")


def solution(mesh):
    return jax.shard_map(
        per_device,
        mesh=mesh,
        in_specs=(
            P("bond", None, None, None),
            P("bond", "mpo", None),
            P("bond", "mpo", None),
            P("mpo", None),
            P("mpo", None),
            P(),
        ),
        out_specs=P("bond", None, None, None),
        check_vma=False,
    )
```

```python
import jax
import jax.numpy as jnp
from jax import lax
from jax.experimental import pallas as pl
from jax.experimental.pallas import tpu as pltpu
from jax.sharding import PartitionSpec as P


def block_kernel(gain_ref, wave_ref, left_ref, *refs):
    right_refs, out_ref = refs[:-1], refs[-1]
    block_count, block_width, column_count = wave_ref.shape
    group_count = left_ref.shape[0]
    term_count = gain_ref.shape[0] // group_count
    vectors = column_count // block_width
    lanes = right_refs[0].shape[2]
    half_rows = block_width // 2
    tile_rows = lax.broadcasted_iota(jnp.int32, (lanes, 2 * column_count), 0)
    tile_cols = lax.broadcasted_iota(jnp.int32, (lanes, 2 * column_count), 1)
    lane_tile = (
        (tile_rows // block_width == tile_cols // column_count)
        & (tile_rows % block_width == tile_cols % block_width)
    ).astype(jnp.bfloat16)
    diag_rows = lax.broadcasted_iota(jnp.int32, (column_count, column_count), 0)
    diag_cols = lax.broadcasted_iota(jnp.int32, (column_count, column_count), 1)
    diagonal = diag_rows // block_width == diag_cols // block_width

    def body(b, carry):
        wave = wave_ref[b]
        total = jnp.zeros((block_width, column_count), jnp.float32)
        for g in range(group_count):
            scaled = []
            for w in range(term_count):
                piece = left_ref[g, w * block_width:(w + 1) * block_width, :]
                gain = gain_ref[g * term_count + w, b]
                scaled.append((piece.astype(jnp.float32) * gain).astype(jnp.bfloat16))
            left_scaled = jnp.concatenate(scaled, axis=0)
            sectioned = jnp.dot(
                left_scaled, wave, preferred_element_type=jnp.float32
            ).astype(jnp.bfloat16)
            tiled = jnp.dot(
                right_refs[g][b], lane_tile, preferred_element_type=jnp.float32
            ).astype(jnp.bfloat16)
            acc = jnp.zeros((block_width, column_count), jnp.float32)
            for w in range(term_count):
                rows_w = tiled[w * half_rows:(w + 1) * half_rows]
                part = jnp.concatenate(
                    [rows_w[:, :column_count], rows_w[:, column_count:]], axis=0
                )
                expanded = jnp.concatenate([part] * vectors, axis=0)
                expanded = jnp.where(diagonal, expanded, jnp.zeros_like(expanded))
                acc = acc + jnp.dot(
                    sectioned[w * block_width:(w + 1) * block_width],
                    expanded,
                    preferred_element_type=jnp.float32,
                )
            total = total + acc.astype(jnp.bfloat16).astype(jnp.float32)
        out_ref[b] = total.astype(out_ref.dtype)
        return carry

    lax.fori_loop(0, block_count, body, 0)


def apply_blocks(gains, wave_rows, left_rows, right_rows):
    right_rows = tuple(right_rows)
    block_count, block_width, column_count = wave_rows.shape
    group_count, rows = left_rows.shape[0], left_rows.shape[1]
    flops = block_count * group_count * (
        2 * 2 * rows * block_width * column_count
        + 2 * rows * column_count * column_count
    )
    bytes_accessed = 2 * (
        2 * wave_rows.size + left_rows.size + sum(r.size for r in right_rows)
    )
    vmem = pltpu.MemorySpace.VMEM if hasattr(pltpu, "MemorySpace") else pltpu.VMEM
    return pl.pallas_call(
        block_kernel,
        out_shape=jax.ShapeDtypeStruct(wave_rows.shape, jnp.bfloat16),
        in_specs=[
            pl.BlockSpec(memory_space=pltpu.SMEM),
            pl.BlockSpec(memory_space=vmem),
            pl.BlockSpec(memory_space=vmem),
        ]
        + [pl.BlockSpec(memory_space=vmem)] * len(right_rows),
        out_specs=pl.BlockSpec(memory_space=vmem),
        cost_estimate=pl.CostEstimate(
            flops=flops, bytes_accessed=bytes_accessed, transcendentals=0
        ),
    )(gains, wave_rows, left_rows, *right_rows)


def shifted(value, shift, count):
    pairs = [(i, (i + shift) % count) for i in range(count)]
    return lax.ppermute(value, "mpo", pairs)


def per_device(wave_blocks, left_env, right_env, mpo_coef, mpo_mask, right_sector):
    sec_local, class_count, block_width, column_count = wave_blocks.shape
    term_local = left_env.shape[1]
    blocks_local = sec_local * class_count
    bond_count = lax.axis_size("bond")
    bond_index = lax.axis_index("bond")
    mpo_count = lax.axis_size("mpo")
    mpo_index = lax.axis_index("mpo")
    half_rows = block_width // 2
    gains = mpo_coef * mpo_mask.astype(jnp.float32)

    requests = right_sector.reshape(bond_count, blocks_local)
    hits = (requests // sec_local) == bond_index
    send_sector = jnp.sum(
        jnp.where(hits, requests % sec_local, 0), axis=1
    ).astype(jnp.int32)
    right_t = jnp.transpose(
        right_env.reshape(sec_local, term_local, block_width, 2, half_rows),
        (0, 1, 4, 3, 2),
    ).reshape(sec_local, term_local * half_rows, 2 * block_width)
    send_right = jnp.take(right_t, send_sector, axis=0, mode="clip")
    got_right = lax.all_to_all(send_right, "bond", split_axis=0, concat_axis=0, tiled=True)

    left_flat = left_env.reshape(sec_local, term_local * half_rows, 2 * block_width)
    left_parts = [lax.dynamic_index_in_dim(left_flat, mpo_index, 0, keepdims=False)]
    gain_parts = [gains]
    for shift in range(1, mpo_count):
        target = (mpo_index + shift) % mpo_count
        left_parts.append(
            shifted(lax.dynamic_index_in_dim(left_flat, target, 0, keepdims=False), shift, mpo_count)
        )
        gain_parts.append(shifted(gains, shift, mpo_count))
    left_rows = jnp.stack(left_parts).reshape(
        mpo_count, term_local * block_width, block_width
    )
    gain_rows = jnp.stack(gain_parts).reshape(mpo_count * term_local, class_count)

    mine = lax.dynamic_slice_in_dim(requests, bond_index, 1, axis=0).reshape(
        sec_local, class_count
    )
    sources = (mine // sec_local).astype(jnp.int32)
    targets = (mpo_index + jnp.arange(mpo_count, dtype=jnp.int32)) % mpo_count
    picked = jnp.take(
        got_right, jnp.take(sources, targets, axis=0).reshape(-1), axis=0, mode="clip"
    ).reshape((mpo_count, class_count) + got_right.shape[1:])
    right_rows = [picked[0]] + [
        shifted(picked[shift], shift, mpo_count) for shift in range(1, mpo_count)
    ]

    wave_rows = lax.dynamic_index_in_dim(wave_blocks, mpo_index, 0, keepdims=False)
    done = apply_blocks(gain_rows, wave_rows, left_rows, right_rows)

    out_parts = [done] + [shifted(done, shift, mpo_count) for shift in range(1, mpo_count)]
    slot = lax.broadcasted_iota(jnp.int32, (mpo_count,) + done.shape, 0)
    full = jnp.broadcast_to(out_parts[0], (mpo_count,) + done.shape)
    for shift in range(1, mpo_count):
        owner = (mpo_index - shift) % mpo_count
        full = jnp.where(slot == owner, out_parts[shift][None], full)
    return full


def solution(mesh):
    return jax.shard_map(
        per_device,
        mesh=mesh,
        in_specs=(
            P("bond", None, None, None),
            P("bond", "mpo", None),
            P("bond", "mpo", None),
            P("mpo", None),
            P("mpo", None),
            P(),
        ),
        out_specs=P("bond", None, None, None),
        check_vma=False,
    )
```

```python
import jax
import jax.numpy as jnp
from jax import lax
from jax.experimental import pallas as pl
from jax.experimental.pallas import tpu as pltpu
from jax.sharding import PartitionSpec as P


def block_kernel(gain_ref, wave_ref, left_ref, right_ref, out_ref):
    block_count, block_width, column_count = wave_ref.shape
    group_count = left_ref.shape[0]
    term_count = gain_ref.shape[0] // group_count
    vectors = column_count // block_width
    lanes = right_ref.shape[3]
    half_rows = block_width // 2
    tile_rows = lax.broadcasted_iota(jnp.int32, (lanes, 2 * column_count), 0)
    tile_cols = lax.broadcasted_iota(jnp.int32, (lanes, 2 * column_count), 1)
    lane_tile = (
        (tile_rows // block_width == tile_cols // column_count)
        & (tile_rows % block_width == tile_cols % block_width)
    ).astype(jnp.bfloat16)
    diag_rows = lax.broadcasted_iota(jnp.int32, (column_count, column_count), 0)
    diag_cols = lax.broadcasted_iota(jnp.int32, (column_count, column_count), 1)
    diagonal = diag_rows // block_width == diag_cols // block_width

    def body(b, carry):
        wave = wave_ref[b]
        total = jnp.zeros((block_width, column_count), jnp.float32)
        for g in range(group_count):
            scaled = []
            for w in range(term_count):
                piece = left_ref[g, w * block_width:(w + 1) * block_width, :]
                gain = gain_ref[g * term_count + w, b]
                scaled.append((piece.astype(jnp.float32) * gain).astype(jnp.bfloat16))
            left_scaled = jnp.concatenate(scaled, axis=0)
            sectioned = jnp.dot(
                left_scaled, wave, preferred_element_type=jnp.float32
            ).astype(jnp.bfloat16)
            tiled = jnp.dot(
                right_ref[g, b], lane_tile, preferred_element_type=jnp.float32
            ).astype(jnp.bfloat16)
            acc = jnp.zeros((block_width, column_count), jnp.float32)
            for w in range(term_count):
                rows_w = tiled[w * half_rows:(w + 1) * half_rows]
                part = jnp.concatenate(
                    [rows_w[:, :column_count], rows_w[:, column_count:]], axis=0
                )
                expanded = jnp.concatenate([part] * vectors, axis=0)
                expanded = jnp.where(diagonal, expanded, jnp.zeros_like(expanded))
                acc = acc + jnp.dot(
                    sectioned[w * block_width:(w + 1) * block_width],
                    expanded,
                    preferred_element_type=jnp.float32,
                )
            total = total + acc.astype(jnp.bfloat16).astype(jnp.float32)
        out_ref[b] = total.astype(out_ref.dtype)
        return carry

    lax.fori_loop(0, block_count, body, 0)


def apply_blocks(gains, wave_rows, left_rows, right_rows):
    block_count, block_width, column_count = wave_rows.shape
    group_count, rows = left_rows.shape[0], left_rows.shape[1]
    flops = block_count * group_count * (
        2 * 2 * rows * block_width * column_count
        + 2 * rows * column_count * column_count
    )
    bytes_accessed = 2 * (
        2 * wave_rows.size + left_rows.size + right_rows.size
    )
    vmem = pltpu.MemorySpace.VMEM if hasattr(pltpu, "MemorySpace") else pltpu.VMEM
    return pl.pallas_call(
        block_kernel,
        out_shape=jax.ShapeDtypeStruct(wave_rows.shape, jnp.bfloat16),
        in_specs=[
            pl.BlockSpec(memory_space=pltpu.SMEM),
            pl.BlockSpec(memory_space=vmem),
            pl.BlockSpec(memory_space=vmem),
            pl.BlockSpec(memory_space=vmem),
        ],
        out_specs=pl.BlockSpec(memory_space=vmem),
        cost_estimate=pl.CostEstimate(
            flops=flops, bytes_accessed=bytes_accessed, transcendentals=0
        ),
    )(gains, wave_rows, left_rows, right_rows)


def mpo_swap(value):
    return lax.all_to_all(value, "mpo", split_axis=0, concat_axis=0, tiled=True)


def per_device(wave_blocks, left_env, right_env, mpo_coef, mpo_mask, right_sector):
    sec_local, class_count, block_width, column_count = wave_blocks.shape
    term_local = left_env.shape[1]
    blocks_local = sec_local * class_count
    bond_count = lax.axis_size("bond")
    bond_index = lax.axis_index("bond")
    mpo_count = lax.axis_size("mpo")
    mpo_index = lax.axis_index("mpo")
    half_rows = block_width // 2
    gains = mpo_coef * mpo_mask.astype(jnp.float32)

    requests = right_sector.reshape(bond_count, blocks_local)
    hits = (requests // sec_local) == bond_index
    send_sector = jnp.sum(
        jnp.where(hits, requests % sec_local, 0), axis=1
    ).astype(jnp.int32)
    right_t = jnp.transpose(
        right_env.reshape(sec_local, term_local, block_width, 2, half_rows),
        (0, 1, 4, 3, 2),
    ).reshape(sec_local, term_local * half_rows, 2 * block_width)
    send_right = jnp.take(right_t, send_sector, axis=0, mode="clip")
    got_right = lax.all_to_all(send_right, "bond", split_axis=0, concat_axis=0, tiled=True)

    left_flat = left_env.reshape(sec_local, term_local * half_rows, 2 * block_width)
    left_rows = mpo_swap(left_flat).reshape(
        mpo_count, term_local * block_width, block_width
    )
    gain_rows = mpo_swap(
        jnp.broadcast_to(gains[None], (mpo_count,) + gains.shape)
    ).reshape(mpo_count * term_local, class_count)

    mine = lax.dynamic_slice_in_dim(requests, bond_index, 1, axis=0).reshape(blocks_local)
    sources = (mine // sec_local).astype(jnp.int32)
    picked = jnp.take(got_right, sources, axis=0, mode="clip").reshape(
        (mpo_count, class_count) + got_right.shape[1:]
    )
    right_rows = mpo_swap(picked)

    wave_rows = lax.dynamic_index_in_dim(wave_blocks, mpo_index, 0, keepdims=False)
    done = apply_blocks(gain_rows, wave_rows, left_rows, right_rows)

    return mpo_swap(jnp.broadcast_to(done[None], (mpo_count,) + done.shape))


def solution(mesh):
    return jax.shard_map(
        per_device,
        mesh=mesh,
        in_specs=(
            P("bond", None, None, None),
            P("bond", "mpo", None),
            P("bond", "mpo", None),
            P("mpo", None),
            P("mpo", None),
            P(),
        ),
        out_specs=P("bond", None, None, None),
        check_vma=False,
    )
```

```python
import jax
import jax.numpy as jnp
from jax import lax
from jax.experimental import pallas as pl
from jax.experimental.pallas import tpu as pltpu
from jax.sharding import PartitionSpec as P


def kernel_tables(lanes, block_width, column_count):
    tile_rows = lax.broadcasted_iota(jnp.int32, (lanes, 2 * column_count), 0)
    tile_cols = lax.broadcasted_iota(jnp.int32, (lanes, 2 * column_count), 1)
    lane_tile = (
        (tile_rows // block_width == tile_cols // column_count)
        & (tile_rows % block_width == tile_cols % block_width)
    ).astype(jnp.bfloat16)
    diag_rows = lax.broadcasted_iota(jnp.int32, (column_count, column_count), 0)
    diag_cols = lax.broadcasted_iota(jnp.int32, (column_count, column_count), 1)
    diagonal = diag_rows // block_width == diag_cols // block_width
    return lane_tile, diagonal


def sectioned_rows(gain_ref, left_ref, g, b, wave, term_count, block_width):
    scaled = []
    for w in range(term_count):
        piece = left_ref[g, w * block_width:(w + 1) * block_width, :]
        gain = gain_ref[g * term_count + w, b]
        scaled.append((piece.astype(jnp.float32) * gain).astype(jnp.bfloat16))
    left_scaled = jnp.concatenate(scaled, axis=0)
    return jnp.dot(left_scaled, wave, preferred_element_type=jnp.float32).astype(
        jnp.bfloat16
    )


def group_part(sectioned, right, lane_tile, diagonal, term_count, block_width, column_count):
    half_rows = block_width // 2
    vectors = column_count // block_width
    tiled = jnp.dot(right, lane_tile, preferred_element_type=jnp.float32).astype(
        jnp.bfloat16
    )
    acc = jnp.zeros((block_width, column_count), jnp.float32)
    for w in range(term_count):
        rows_w = tiled[w * half_rows:(w + 1) * half_rows]
        part = jnp.concatenate(
            [rows_w[:, :column_count], rows_w[:, column_count:]], axis=0
        )
        expanded = jnp.concatenate([part] * vectors, axis=0)
        expanded = jnp.where(diagonal, expanded, jnp.zeros_like(expanded))
        acc = acc + jnp.dot(
            sectioned[w * block_width:(w + 1) * block_width],
            expanded,
            preferred_element_type=jnp.float32,
        )
    return acc.astype(jnp.bfloat16)


def first_kernel(gain_ref, wave_ref, left_ref, right_ref, sect_ref, own_ref):
    block_count, block_width, column_count = wave_ref.shape
    group_count = left_ref.shape[0]
    term_count = gain_ref.shape[0] // group_count
    lane_tile, diagonal = kernel_tables(right_ref.shape[2], block_width, column_count)

    def body(b, carry):
        wave = wave_ref[b]
        for g in range(group_count):
            sectioned = sectioned_rows(
                gain_ref, left_ref, g, b, wave, term_count, block_width
            )
            if g == 0:
                own_ref[b] = group_part(
                    sectioned, right_ref[b], lane_tile, diagonal,
                    term_count, block_width, column_count,
                )
            else:
                sect_ref[b, g - 1] = sectioned
        return carry

    lax.fori_loop(0, block_count, body, 0)


def second_kernel(sect_ref, own_ref, *refs):
    right_refs, out_ref = refs[:-1], refs[-1]
    block_count, block_width, column_count = own_ref.shape
    term_count = sect_ref.shape[2] // block_width
    lane_tile, diagonal = kernel_tables(right_refs[0].shape[2], block_width, column_count)

    def body(b, carry):
        total = own_ref[b].astype(jnp.float32)
        for g, right_ref in enumerate(right_refs):
            total = total + group_part(
                sect_ref[b, g], right_ref[b], lane_tile, diagonal,
                term_count, block_width, column_count,
            ).astype(jnp.float32)
        out_ref[b] = total.astype(out_ref.dtype)
        return carry

    lax.fori_loop(0, block_count, body, 0)


def vmem_specs(count):
    vmem = pltpu.MemorySpace.VMEM if hasattr(pltpu, "MemorySpace") else pltpu.VMEM
    return [pl.BlockSpec(memory_space=vmem)] * count


def apply_blocks(gains, wave_rows, left_rows, right_rows):
    block_count, block_width, column_count = wave_rows.shape
    group_count, rows = left_rows.shape[0], left_rows.shape[1]
    section_flops = 2 * rows * block_width * column_count
    part_flops = 2 * rows * block_width * column_count + 2 * rows * column_count * column_count
    sect_shape = (block_count, group_count - 1, rows, column_count)
    sectioned, own = pl.pallas_call(
        first_kernel,
        out_shape=(
            jax.ShapeDtypeStruct(sect_shape, jnp.bfloat16),
            jax.ShapeDtypeStruct(wave_rows.shape, jnp.bfloat16),
        ),
        in_specs=[pl.BlockSpec(memory_space=pltpu.SMEM)] + vmem_specs(3),
        out_specs=tuple(vmem_specs(2)),
        cost_estimate=pl.CostEstimate(
            flops=block_count * (group_count * section_flops + part_flops),
            bytes_accessed=2 * (wave_rows.size * 2 + left_rows.size + right_rows[0].size
                                + block_count * (group_count - 1) * rows * column_count),
            transcendentals=0,
        ),
    )(gains, wave_rows, left_rows, right_rows[0])
    remote = tuple(right_rows[1:])
    return pl.pallas_call(
        second_kernel,
        out_shape=jax.ShapeDtypeStruct(wave_rows.shape, jnp.bfloat16),
        in_specs=vmem_specs(2 + len(remote)),
        out_specs=vmem_specs(1)[0],
        cost_estimate=pl.CostEstimate(
            flops=block_count * len(remote) * part_flops,
            bytes_accessed=2 * (sectioned.size + 2 * own.size + sum(r.size for r in remote)),
            transcendentals=0,
        ),
    )(sectioned, own, *remote)


def shifted(value, shift, count):
    pairs = [(i, (i + shift) % count) for i in range(count)]
    return lax.ppermute(value, "mpo", pairs)


def per_device(wave_blocks, left_env, right_env, mpo_coef, mpo_mask, right_sector):
    sec_local, class_count, block_width, column_count = wave_blocks.shape
    term_local = left_env.shape[1]
    blocks_local = sec_local * class_count
    bond_count = lax.axis_size("bond")
    bond_index = lax.axis_index("bond")
    mpo_count = lax.axis_size("mpo")
    mpo_index = lax.axis_index("mpo")
    half_rows = block_width // 2
    gains = mpo_coef * mpo_mask.astype(jnp.float32)

    requests = right_sector.reshape(bond_count, blocks_local)
    hits = (requests // sec_local) == bond_index
    send_sector = jnp.sum(
        jnp.where(hits, requests % sec_local, 0), axis=1
    ).astype(jnp.int32)
    right_t = jnp.transpose(
        right_env.reshape(sec_local, term_local, block_width, 2, half_rows),
        (0, 1, 4, 3, 2),
    ).reshape(sec_local, term_local * half_rows, 2 * block_width)
    send_right = jnp.take(right_t, send_sector, axis=0, mode="clip")
    got_right = lax.all_to_all(send_right, "bond", split_axis=0, concat_axis=0, tiled=True)

    left_flat = left_env.reshape(sec_local, term_local * half_rows, 2 * block_width)
    left_parts = [lax.dynamic_index_in_dim(left_flat, mpo_index, 0, keepdims=False)]
    gain_parts = [gains]
    for shift in range(1, mpo_count):
        target = (mpo_index + shift) % mpo_count
        left_parts.append(
            shifted(lax.dynamic_index_in_dim(left_flat, target, 0, keepdims=False), shift, mpo_count)
        )
        gain_parts.append(shifted(gains, shift, mpo_count))
    left_rows = jnp.stack(left_parts).reshape(
        mpo_count, term_local * block_width, block_width
    )
    gain_rows = jnp.stack(gain_parts).reshape(mpo_count * term_local, class_count)

    mine = lax.dynamic_slice_in_dim(requests, bond_index, 1, axis=0).reshape(
        sec_local, class_count
    )
    sources = (mine // sec_local).astype(jnp.int32)
    targets = (mpo_index + jnp.arange(mpo_count, dtype=jnp.int32)) % mpo_count
    picked = jnp.take(
        got_right, jnp.take(sources, targets, axis=0).reshape(-1), axis=0, mode="clip"
    ).reshape((mpo_count, class_count) + got_right.shape[1:])
    right_rows = [picked[0]] + [
        shifted(picked[shift], shift, mpo_count) for shift in range(1, mpo_count)
    ]

    wave_rows = lax.dynamic_index_in_dim(wave_blocks, mpo_index, 0, keepdims=False)
    done = apply_blocks(gain_rows, wave_rows, left_rows, right_rows)

    out_parts = [done] + [shifted(done, shift, mpo_count) for shift in range(1, mpo_count)]
    slot = lax.broadcasted_iota(jnp.int32, (mpo_count,) + done.shape, 0)
    full = jnp.broadcast_to(out_parts[0], (mpo_count,) + done.shape)
    for shift in range(1, mpo_count):
        owner = (mpo_index - shift) % mpo_count
        full = jnp.where(slot == owner, out_parts[shift][None], full)
    return full


def solution(mesh):
    return jax.shard_map(
        per_device,
        mesh=mesh,
        in_specs=(
            P("bond", None, None, None),
            P("bond", "mpo", None),
            P("bond", "mpo", None),
            P("mpo", None),
            P("mpo", None),
            P(),
        ),
        out_specs=P("bond", None, None, None),
        check_vma=False,
    )
```

```python
import jax
import jax.numpy as jnp
from jax import lax
from jax.experimental import pallas as pl
from jax.experimental.pallas import tpu as pltpu
from jax.sharding import PartitionSpec as P


def block_kernel(gain_ref, wave_ref, left_ref, *refs):
    right_refs, out_ref = refs[:-1], refs[-1]
    block_count, block_width, column_count = wave_ref.shape
    group_count = left_ref.shape[0]
    term_count = gain_ref.shape[0] // group_count
    vectors = column_count // block_width
    lanes = right_refs[0].shape[2]
    half_rows = block_width // 2
    tile_rows = lax.broadcasted_iota(jnp.int32, (lanes, 2 * column_count), 0)
    tile_cols = lax.broadcasted_iota(jnp.int32, (lanes, 2 * column_count), 1)
    lane_tile = (
        (tile_rows // block_width == tile_cols // column_count)
        & (tile_rows % block_width == tile_cols % block_width)
    ).astype(jnp.bfloat16)
    diag_rows = lax.broadcasted_iota(jnp.int32, (column_count, column_count), 0)
    diag_cols = lax.broadcasted_iota(jnp.int32, (column_count, column_count), 1)
    diagonal = diag_rows // block_width == diag_cols // block_width

    def body(b, carry):
        wave = wave_ref[b]
        total = jnp.zeros((block_width, column_count), jnp.float32)
        for g in range(group_count):
            right = right_refs[g]

            def term(w, acc):
                gain = gain_ref[g * term_count + w, b]

                def live(acc):
                    piece = left_ref[g, pl.ds(w * block_width, block_width), :]
                    scaled = (piece.astype(jnp.float32) * gain).astype(jnp.bfloat16)
                    sectioned = jnp.dot(
                        scaled, wave, preferred_element_type=jnp.float32
                    ).astype(jnp.bfloat16)
                    rows_w = jnp.dot(
                        right[b, pl.ds(w * half_rows, half_rows), :],
                        lane_tile,
                        preferred_element_type=jnp.float32,
                    ).astype(jnp.bfloat16)
                    part = jnp.concatenate(
                        [rows_w[:, :column_count], rows_w[:, column_count:]], axis=0
                    )
                    expanded = jnp.concatenate([part] * vectors, axis=0)
                    expanded = jnp.where(diagonal, expanded, jnp.zeros_like(expanded))
                    return acc + jnp.dot(
                        sectioned, expanded, preferred_element_type=jnp.float32
                    )

                return lax.cond(gain != 0.0, live, lambda acc: acc, acc)

            acc = jnp.zeros((block_width, column_count), jnp.float32)
            for w in range(term_count):
                acc = term(w, acc)
            total = total + acc.astype(jnp.bfloat16).astype(jnp.float32)
        out_ref[b] = total.astype(out_ref.dtype)
        return carry

    lax.fori_loop(0, block_count, body, 0)


def apply_blocks(gains, wave_rows, left_rows, right_rows):
    right_rows = tuple(right_rows)
    block_count, block_width, column_count = wave_rows.shape
    group_count, rows = left_rows.shape[0], left_rows.shape[1]
    flops = block_count * group_count * (
        2 * 2 * rows * block_width * column_count
        + 2 * rows * column_count * column_count
    )
    bytes_accessed = 2 * (
        2 * wave_rows.size + left_rows.size + sum(r.size for r in right_rows)
    )
    vmem = pltpu.MemorySpace.VMEM if hasattr(pltpu, "MemorySpace") else pltpu.VMEM
    return pl.pallas_call(
        block_kernel,
        out_shape=jax.ShapeDtypeStruct(wave_rows.shape, jnp.bfloat16),
        in_specs=[
            pl.BlockSpec(memory_space=pltpu.SMEM),
            pl.BlockSpec(memory_space=vmem),
            pl.BlockSpec(memory_space=vmem),
        ]
        + [pl.BlockSpec(memory_space=vmem)] * len(right_rows),
        out_specs=pl.BlockSpec(memory_space=vmem),
        cost_estimate=pl.CostEstimate(
            flops=flops, bytes_accessed=bytes_accessed, transcendentals=0
        ),
    )(gains, wave_rows, left_rows, *right_rows)


def shifted(value, shift, count):
    pairs = [(i, (i + shift) % count) for i in range(count)]
    return lax.ppermute(value, "mpo", pairs)


def per_device(wave_blocks, left_env, right_env, mpo_coef, mpo_mask, right_sector):
    sec_local, class_count, block_width, column_count = wave_blocks.shape
    term_local = left_env.shape[1]
    blocks_local = sec_local * class_count
    bond_count = lax.axis_size("bond")
    bond_index = lax.axis_index("bond")
    mpo_count = lax.axis_size("mpo")
    mpo_index = lax.axis_index("mpo")
    half_rows = block_width // 2
    gains = mpo_coef * mpo_mask.astype(jnp.float32)

    requests = right_sector.reshape(bond_count, blocks_local)
    hits = (requests // sec_local) == bond_index
    send_sector = jnp.sum(
        jnp.where(hits, requests % sec_local, 0), axis=1
    ).astype(jnp.int32)
    right_t = jnp.transpose(
        right_env.reshape(sec_local, term_local, block_width, 2, half_rows),
        (0, 1, 4, 3, 2),
    ).reshape(sec_local, term_local * half_rows, 2 * block_width)
    send_right = jnp.take(right_t, send_sector, axis=0, mode="clip")
    got_right = lax.all_to_all(send_right, "bond", split_axis=0, concat_axis=0, tiled=True)

    left_flat = left_env.reshape(sec_local, term_local * half_rows, 2 * block_width)
    left_parts = [lax.dynamic_index_in_dim(left_flat, mpo_index, 0, keepdims=False)]
    gain_parts = [gains]
    for shift in range(1, mpo_count):
        target = (mpo_index + shift) % mpo_count
        left_parts.append(
            shifted(lax.dynamic_index_in_dim(left_flat, target, 0, keepdims=False), shift, mpo_count)
        )
        gain_parts.append(shifted(gains, shift, mpo_count))
    left_rows = jnp.stack(left_parts).reshape(
        mpo_count, term_local * block_width, block_width
    )
    gain_rows = jnp.stack(gain_parts).reshape(mpo_count * term_local, class_count)

    mine = lax.dynamic_slice_in_dim(requests, bond_index, 1, axis=0).reshape(
        sec_local, class_count
    )
    sources = (mine // sec_local).astype(jnp.int32)
    targets = (mpo_index + jnp.arange(mpo_count, dtype=jnp.int32)) % mpo_count
    picked = jnp.take(
        got_right, jnp.take(sources, targets, axis=0).reshape(-1), axis=0, mode="clip"
    ).reshape((mpo_count, class_count) + got_right.shape[1:])
    right_rows = [picked[0]] + [
        shifted(picked[shift], shift, mpo_count) for shift in range(1, mpo_count)
    ]

    wave_rows = lax.dynamic_index_in_dim(wave_blocks, mpo_index, 0, keepdims=False)
    done = apply_blocks(gain_rows, wave_rows, left_rows, right_rows)

    out_parts = [done] + [shifted(done, shift, mpo_count) for shift in range(1, mpo_count)]
    slot = lax.broadcasted_iota(jnp.int32, (mpo_count,) + done.shape, 0)
    full = jnp.broadcast_to(out_parts[0], (mpo_count,) + done.shape)
    for shift in range(1, mpo_count):
        owner = (mpo_index - shift) % mpo_count
        full = jnp.where(slot == owner, out_parts[shift][None], full)
    return full


def solution(mesh):
    return jax.shard_map(
        per_device,
        mesh=mesh,
        in_specs=(
            P("bond", None, None, None),
            P("bond", "mpo", None),
            P("bond", "mpo", None),
            P("mpo", None),
            P("mpo", None),
            P(),
        ),
        out_specs=P("bond", None, None, None),
        check_vma=False,
    )
```

```python
import jax
import jax.numpy as jnp
from jax import lax
from jax.experimental import pallas as pl
from jax.experimental.pallas import tpu as pltpu
from jax.sharding import PartitionSpec as P


def block_kernel(gain_ref, wave_ref, left_ref, *refs):
    right_refs, out_ref, tiled_ref = refs[:-2], refs[-2], refs[-1]
    block_count, block_width, column_count = wave_ref.shape
    group_count = left_ref.shape[0]
    term_count = gain_ref.shape[0] // group_count
    vectors = column_count // block_width
    lanes = right_refs[0].shape[2]
    half_rows = block_width // 2
    tile_rows = lax.broadcasted_iota(jnp.int32, (lanes, 2 * column_count), 0)
    tile_cols = lax.broadcasted_iota(jnp.int32, (lanes, 2 * column_count), 1)
    lane_tile = (
        (tile_rows // block_width == tile_cols // column_count)
        & (tile_rows % block_width == tile_cols % block_width)
    ).astype(jnp.bfloat16)
    diag_rows = lax.broadcasted_iota(jnp.int32, (column_count, column_count), 0)
    diag_cols = lax.broadcasted_iota(jnp.int32, (column_count, column_count), 1)
    diagonal = diag_rows // block_width == diag_cols // block_width

    right_rows = right_refs[0].shape[1]
    for g, right_ref in enumerate(right_refs):
        flat = right_ref[...].reshape(block_count * right_rows, lanes)
        tiled_ref[g] = jnp.dot(
            flat, lane_tile, preferred_element_type=jnp.float32
        ).astype(jnp.bfloat16)

    def body(b, carry):
        wave = wave_ref[b]
        total = jnp.zeros((block_width, column_count), jnp.float32)
        for g in range(group_count):
            scaled = []
            for w in range(term_count):
                piece = left_ref[g, w * block_width:(w + 1) * block_width, :]
                gain = gain_ref[g * term_count + w, b]
                scaled.append((piece.astype(jnp.float32) * gain).astype(jnp.bfloat16))
            left_scaled = jnp.concatenate(scaled, axis=0)
            sectioned = jnp.dot(
                left_scaled, wave, preferred_element_type=jnp.float32
            ).astype(jnp.bfloat16)
            tiled = tiled_ref[g, pl.ds(pl.multiple_of(b * right_rows, right_rows), right_rows), :]
            acc = jnp.zeros((block_width, column_count), jnp.float32)
            for w in range(term_count):
                rows_w = tiled[w * half_rows:(w + 1) * half_rows]
                part = jnp.concatenate(
                    [rows_w[:, :column_count], rows_w[:, column_count:]], axis=0
                )
                expanded = jnp.concatenate([part] * vectors, axis=0)
                expanded = jnp.where(diagonal, expanded, jnp.zeros_like(expanded))
                acc = acc + jnp.dot(
                    sectioned[w * block_width:(w + 1) * block_width],
                    expanded,
                    preferred_element_type=jnp.float32,
                )
            total = total + acc.astype(jnp.bfloat16).astype(jnp.float32)
        out_ref[b] = total.astype(out_ref.dtype)
        return carry

    lax.fori_loop(0, block_count, body, 0)


def apply_blocks(gains, wave_rows, left_rows, right_rows):
    right_rows = tuple(right_rows)
    block_count, block_width, column_count = wave_rows.shape
    group_count, rows = left_rows.shape[0], left_rows.shape[1]
    flops = block_count * group_count * (
        2 * 2 * rows * block_width * column_count
        + 2 * rows * column_count * column_count
    )
    bytes_accessed = 2 * (
        2 * wave_rows.size + left_rows.size + sum(r.size for r in right_rows)
    )
    vmem = pltpu.MemorySpace.VMEM if hasattr(pltpu, "MemorySpace") else pltpu.VMEM
    return pl.pallas_call(
        block_kernel,
        out_shape=jax.ShapeDtypeStruct(wave_rows.shape, jnp.bfloat16),
        in_specs=[
            pl.BlockSpec(memory_space=pltpu.SMEM),
            pl.BlockSpec(memory_space=vmem),
            pl.BlockSpec(memory_space=vmem),
        ]
        + [pl.BlockSpec(memory_space=vmem)] * len(right_rows),
        out_specs=pl.BlockSpec(memory_space=vmem),
        scratch_shapes=[
            pltpu.VMEM(
                (group_count, block_count * right_rows[0].shape[1], 4 * right_rows[0].shape[2]),
                jnp.bfloat16,
            )
        ],
        cost_estimate=pl.CostEstimate(
            flops=flops, bytes_accessed=bytes_accessed, transcendentals=0
        ),
    )(gains, wave_rows, left_rows, *right_rows)


def shifted(value, shift, count):
    pairs = [(i, (i + shift) % count) for i in range(count)]
    return lax.ppermute(value, "mpo", pairs)


def per_device(wave_blocks, left_env, right_env, mpo_coef, mpo_mask, right_sector):
    sec_local, class_count, block_width, column_count = wave_blocks.shape
    term_local = left_env.shape[1]
    blocks_local = sec_local * class_count
    bond_count = lax.axis_size("bond")
    bond_index = lax.axis_index("bond")
    mpo_count = lax.axis_size("mpo")
    mpo_index = lax.axis_index("mpo")
    half_rows = block_width // 2
    gains = mpo_coef * mpo_mask.astype(jnp.float32)

    requests = right_sector.reshape(bond_count, blocks_local)
    hits = (requests // sec_local) == bond_index
    send_sector = jnp.sum(
        jnp.where(hits, requests % sec_local, 0), axis=1
    ).astype(jnp.int32)
    right_t = jnp.transpose(
        right_env.reshape(sec_local, term_local, block_width, 2, half_rows),
        (0, 1, 4, 3, 2),
    ).reshape(sec_local, term_local * half_rows, 2 * block_width)
    send_right = jnp.take(right_t, send_sector, axis=0, mode="clip")
    got_right = lax.all_to_all(send_right, "bond", split_axis=0, concat_axis=0, tiled=True)

    left_flat = left_env.reshape(sec_local, term_local * half_rows, 2 * block_width)
    left_parts = [lax.dynamic_index_in_dim(left_flat, mpo_index, 0, keepdims=False)]
    gain_parts = [gains]
    for shift in range(1, mpo_count):
        target = (mpo_index + shift) % mpo_count
        left_parts.append(
            shifted(lax.dynamic_index_in_dim(left_flat, target, 0, keepdims=False), shift, mpo_count)
        )
        gain_parts.append(shifted(gains, shift, mpo_count))
    left_rows = jnp.stack(left_parts).reshape(
        mpo_count, term_local * block_width, block_width
    )
    gain_rows = jnp.stack(gain_parts).reshape(mpo_count * term_local, class_count)

    mine = lax.dynamic_slice_in_dim(requests, bond_index, 1, axis=0).reshape(
        sec_local, class_count
    )
    sources = (mine // sec_local).astype(jnp.int32)
    targets = (mpo_index + jnp.arange(mpo_count, dtype=jnp.int32)) % mpo_count
    picked = jnp.take(
        got_right, jnp.take(sources, targets, axis=0).reshape(-1), axis=0, mode="clip"
    ).reshape((mpo_count, class_count) + got_right.shape[1:])
    right_rows = [picked[0]] + [
        shifted(picked[shift], shift, mpo_count) for shift in range(1, mpo_count)
    ]

    wave_rows = lax.dynamic_index_in_dim(wave_blocks, mpo_index, 0, keepdims=False)
    done = apply_blocks(gain_rows, wave_rows, left_rows, right_rows)

    out_parts = [done] + [shifted(done, shift, mpo_count) for shift in range(1, mpo_count)]
    full = jnp.zeros((mpo_count,) + done.shape, done.dtype)
    for shift in range(mpo_count):
        owner = (mpo_index - shift) % mpo_count
        full = lax.dynamic_update_index_in_dim(full, out_parts[shift], owner, 0)
    return full


def solution(mesh):
    return jax.shard_map(
        per_device,
        mesh=mesh,
        in_specs=(
            P("bond", None, None, None),
            P("bond", "mpo", None),
            P("bond", "mpo", None),
            P("mpo", None),
            P("mpo", None),
            P(),
        ),
        out_specs=P("bond", None, None, None),
        check_vma=False,
    )
```

```python
import jax
import jax.numpy as jnp
from jax import lax
from jax.experimental import pallas as pl
from jax.experimental.pallas import tpu as pltpu
from jax.sharding import PartitionSpec as P


def block_kernel(gain_ref, wave_ref, left_ref, *refs):
    right_ref, out_ref, tiled_ref = refs
    block_count, block_width, column_count = wave_ref.shape
    group_count = left_ref.shape[0]
    term_count = gain_ref.shape[0] // group_count
    vectors = column_count // block_width
    lanes = right_ref.shape[3]
    half_rows = block_width // 2
    tile_rows = lax.broadcasted_iota(jnp.int32, (lanes, 2 * column_count), 0)
    tile_cols = lax.broadcasted_iota(jnp.int32, (lanes, 2 * column_count), 1)
    lane_tile = (
        (tile_rows // block_width == tile_cols // column_count)
        & (tile_rows % block_width == tile_cols % block_width)
    ).astype(jnp.bfloat16)
    diag_rows = lax.broadcasted_iota(jnp.int32, (column_count, column_count), 0)
    diag_cols = lax.broadcasted_iota(jnp.int32, (column_count, column_count), 1)
    diagonal = diag_rows // block_width == diag_cols // block_width

    right_rows = right_ref.shape[2]
    for g in range(group_count):
        flat = right_ref[g].reshape(block_count * right_rows, lanes)
        tiled_ref[g] = jnp.dot(
            flat, lane_tile, preferred_element_type=jnp.float32
        ).astype(jnp.bfloat16)

    def body(b, carry):
        wave = wave_ref[b]
        total = jnp.zeros((block_width, column_count), jnp.float32)
        for g in range(group_count):
            scaled = []
            for w in range(term_count):
                piece = left_ref[g, w * block_width:(w + 1) * block_width, :]
                gain = gain_ref[g * term_count + w, b]
                scaled.append((piece.astype(jnp.float32) * gain).astype(jnp.bfloat16))
            left_scaled = jnp.concatenate(scaled, axis=0)
            sectioned = jnp.dot(
                left_scaled, wave, preferred_element_type=jnp.float32
            ).astype(jnp.bfloat16)
            tiled = tiled_ref[g, pl.ds(pl.multiple_of(b * right_rows, right_rows), right_rows), :]
            acc = jnp.zeros((block_width, column_count), jnp.float32)
            for w in range(term_count):
                rows_w = tiled[w * half_rows:(w + 1) * half_rows]
                part = jnp.concatenate(
                    [rows_w[:, :column_count], rows_w[:, column_count:]], axis=0
                )
                expanded = jnp.concatenate([part] * vectors, axis=0)
                expanded = jnp.where(diagonal, expanded, jnp.zeros_like(expanded))
                acc = acc + jnp.dot(
                    sectioned[w * block_width:(w + 1) * block_width],
                    expanded,
                    preferred_element_type=jnp.float32,
                )
            total = total + acc.astype(jnp.bfloat16).astype(jnp.float32)
        out_ref[b] = total.astype(out_ref.dtype)
        return carry

    lax.fori_loop(0, block_count, body, 0)


def apply_blocks(gains, wave_rows, left_rows, right_rows):
    block_count, block_width, column_count = wave_rows.shape
    group_count, rows = left_rows.shape[0], left_rows.shape[1]
    flops = block_count * group_count * (
        2 * 2 * rows * block_width * column_count
        + 2 * rows * column_count * column_count
    )
    bytes_accessed = 2 * (
        2 * wave_rows.size + left_rows.size + right_rows.size
    )
    vmem = pltpu.MemorySpace.VMEM if hasattr(pltpu, "MemorySpace") else pltpu.VMEM
    return pl.pallas_call(
        block_kernel,
        out_shape=jax.ShapeDtypeStruct(wave_rows.shape, jnp.bfloat16),
        in_specs=[
            pl.BlockSpec(memory_space=pltpu.SMEM),
            pl.BlockSpec(memory_space=vmem),
            pl.BlockSpec(memory_space=vmem),
            pl.BlockSpec(memory_space=vmem),
        ],
        out_specs=pl.BlockSpec(memory_space=vmem),
        scratch_shapes=[
            pltpu.VMEM(
                (group_count, block_count * right_rows.shape[2], 4 * right_rows.shape[3]),
                jnp.bfloat16,
            )
        ],
        cost_estimate=pl.CostEstimate(
            flops=flops, bytes_accessed=bytes_accessed, transcendentals=0
        ),
    )(gains, wave_rows, left_rows, right_rows)


def shifted(value, shift, count):
    pairs = [(i, (i + shift) % count) for i in range(count)]
    return lax.ppermute(value, "mpo", pairs)


def per_device(wave_blocks, left_env, right_env, mpo_coef, mpo_mask, right_sector):
    sec_local, class_count, block_width, column_count = wave_blocks.shape
    term_local = left_env.shape[1]
    blocks_local = sec_local * class_count
    bond_count = lax.axis_size("bond")
    bond_index = lax.axis_index("bond")
    mpo_count = lax.axis_size("mpo")
    mpo_index = lax.axis_index("mpo")
    half_rows = block_width // 2
    gains = mpo_coef * mpo_mask.astype(jnp.float32)

    requests = right_sector.reshape(bond_count, blocks_local)
    hits = (requests // sec_local) == bond_index
    send_sector = jnp.sum(
        jnp.where(hits, requests % sec_local, 0), axis=1
    ).astype(jnp.int32)
    right_t = jnp.transpose(
        right_env.reshape(sec_local, term_local, block_width, 2, half_rows),
        (0, 1, 4, 3, 2),
    ).reshape(sec_local, term_local * half_rows, 2 * block_width)
    send_right = jnp.take(right_t, send_sector, axis=0, mode="clip")
    got_right = lax.all_to_all(send_right, "bond", split_axis=0, concat_axis=0, tiled=True)

    left_flat = left_env.reshape(sec_local, term_local * half_rows, 2 * block_width)
    left_parts = [lax.dynamic_index_in_dim(left_flat, mpo_index, 0, keepdims=False)]
    gain_parts = [gains]
    for shift in range(1, mpo_count):
        target = (mpo_index + shift) % mpo_count
        left_parts.append(
            shifted(lax.dynamic_index_in_dim(left_flat, target, 0, keepdims=False), shift, mpo_count)
        )
        gain_parts.append(shifted(gains, shift, mpo_count))
    groups = (mpo_index - jnp.arange(mpo_count, dtype=jnp.int32)) % mpo_count
    left_rows = jnp.take(jnp.stack(left_parts), groups, axis=0, mode="clip").reshape(
        mpo_count, term_local * block_width, block_width
    )
    gain_rows = jnp.take(jnp.stack(gain_parts), groups, axis=0, mode="clip").reshape(
        mpo_count * term_local, class_count
    )

    mine = lax.dynamic_slice_in_dim(requests, bond_index, 1, axis=0).reshape(
        sec_local, class_count
    )
    sources = (mine // sec_local).astype(jnp.int32)
    picked = jnp.take(got_right, sources.reshape(-1), axis=0, mode="clip").reshape(
        (mpo_count, class_count) + got_right.shape[1:]
    )
    by_group = lax.all_to_all(picked, "mpo", split_axis=0, concat_axis=0, tiled=True)
    right_rows = by_group

    wave_rows = lax.dynamic_index_in_dim(wave_blocks, mpo_index, 0, keepdims=False)
    done = apply_blocks(gain_rows, wave_rows, left_rows, right_rows)

    out_parts = [done] + [shifted(done, shift, mpo_count) for shift in range(1, mpo_count)]
    full = jnp.zeros((mpo_count,) + done.shape, done.dtype)
    for shift in range(mpo_count):
        owner = (mpo_index - shift) % mpo_count
        full = lax.dynamic_update_index_in_dim(full, out_parts[shift], owner, 0)
    return full


def solution(mesh):
    return jax.shard_map(
        per_device,
        mesh=mesh,
        in_specs=(
            P("bond", None, None, None),
            P("bond", "mpo", None),
            P("bond", "mpo", None),
            P("mpo", None),
            P("mpo", None),
            P(),
        ),
        out_specs=P("bond", None, None, None),
        check_vma=False,
    )
```

```python
import jax
import jax.numpy as jnp
from jax import lax
from jax.experimental import pallas as pl
from jax.experimental.pallas import tpu as pltpu
from jax.sharding import PartitionSpec as P


def block_kernel(gain_ref, wave_ref, left_ref, *refs):
    right_refs, out_ref, tiled_ref = refs[:-2], refs[-2], refs[-1]
    block_count, block_width, column_count = wave_ref.shape
    group_count = left_ref.shape[0]
    term_count = gain_ref.shape[0] // group_count
    vectors = column_count // block_width
    lanes = right_refs[0].shape[2]
    half_rows = block_width // 2
    tile_rows = lax.broadcasted_iota(jnp.int32, (lanes, 2 * column_count), 0)
    tile_cols = lax.broadcasted_iota(jnp.int32, (lanes, 2 * column_count), 1)
    lane_tile = (
        (tile_rows // block_width == tile_cols // column_count)
        & (tile_rows % block_width == tile_cols % block_width)
    ).astype(jnp.bfloat16)
    diag_rows = lax.broadcasted_iota(jnp.int32, (column_count, column_count), 0)
    diag_cols = lax.broadcasted_iota(jnp.int32, (column_count, column_count), 1)
    diagonal = diag_rows // block_width == diag_cols // block_width

    right_rows = right_refs[0].shape[1]
    for g, right_ref in enumerate(right_refs):
        flat = right_ref[...].reshape(block_count * right_rows, lanes)
        tiled_ref[g] = jnp.dot(
            flat, lane_tile, preferred_element_type=jnp.float32
        ).astype(jnp.bfloat16)

    def body(b, carry):
        wave = wave_ref[b]
        total = jnp.zeros((block_width, column_count), jnp.float32)
        for g in range(group_count):
            scaled = []
            for w in range(term_count):
                piece = left_ref[g, w * block_width:(w + 1) * block_width, :]
                gain = gain_ref[g * term_count + w, b]
                scaled.append((piece.astype(jnp.float32) * gain).astype(jnp.bfloat16))
            left_scaled = jnp.concatenate(scaled, axis=0)
            sectioned = jnp.dot(
                left_scaled, wave, preferred_element_type=jnp.float32
            ).astype(jnp.bfloat16)
            tiled = tiled_ref[g, pl.ds(pl.multiple_of(b * right_rows, right_rows), right_rows), :]
            acc = jnp.zeros((block_width, column_count), jnp.float32)
            for w in range(term_count):
                rows_w = tiled[w * half_rows:(w + 1) * half_rows]
                part = jnp.concatenate(
                    [rows_w[:, :column_count], rows_w[:, column_count:]], axis=0
                )
                expanded = jnp.concatenate([part] * vectors, axis=0)
                expanded = jnp.where(diagonal, expanded, jnp.zeros_like(expanded))
                acc = acc + jnp.dot(
                    sectioned[w * block_width:(w + 1) * block_width],
                    expanded,
                    preferred_element_type=jnp.float32,
                )
            total = total + acc.astype(jnp.bfloat16).astype(jnp.float32)
        out_ref[b] = total.astype(out_ref.dtype)
        return carry

    lax.fori_loop(0, block_count, body, 0)


def apply_blocks(gains, wave_rows, left_rows, right_rows):
    right_rows = tuple(right_rows)
    block_count, block_width, column_count = wave_rows.shape
    group_count, rows = left_rows.shape[0], left_rows.shape[1]
    flops = block_count * group_count * (
        2 * 2 * rows * block_width * column_count
        + 2 * rows * column_count * column_count
    )
    bytes_accessed = 2 * (
        2 * wave_rows.size + left_rows.size + sum(r.size for r in right_rows)
    )
    vmem = pltpu.MemorySpace.VMEM if hasattr(pltpu, "MemorySpace") else pltpu.VMEM
    return pl.pallas_call(
        block_kernel,
        out_shape=jax.ShapeDtypeStruct(wave_rows.shape, jnp.bfloat16),
        in_specs=[
            pl.BlockSpec(memory_space=pltpu.SMEM),
            pl.BlockSpec(memory_space=vmem),
            pl.BlockSpec(memory_space=vmem),
        ]
        + [pl.BlockSpec(memory_space=vmem)] * len(right_rows),
        out_specs=pl.BlockSpec(memory_space=vmem),
        scratch_shapes=[
            pltpu.VMEM(
                (group_count, block_count * right_rows[0].shape[1], 4 * right_rows[0].shape[2]),
                jnp.bfloat16,
            )
        ],
        cost_estimate=pl.CostEstimate(
            flops=flops, bytes_accessed=bytes_accessed, transcendentals=0
        ),
    )(gains, wave_rows, left_rows, *right_rows)


def shifted(value, shift, count):
    pairs = [(i, (i + shift) % count) for i in range(count)]
    return lax.ppermute(value, "mpo", pairs)


def per_device_body(wave_blocks, left_env, right_env, mpo_coef, mpo_mask, right_sector):
    sec_local, class_count, block_width, _ = wave_blocks.shape
    term_local = left_env.shape[1]
    blocks_local = sec_local * class_count
    bond_count = lax.axis_size("bond")
    bond_index = lax.axis_index("bond")
    mpo_count = lax.axis_size("mpo")
    mpo_index = lax.axis_index("mpo")
    half_rows = block_width // 2
    gains = mpo_coef * mpo_mask.astype(jnp.float32)

    requests = right_sector.reshape(bond_count, blocks_local)
    hits = (requests // sec_local) == bond_index
    send_sector = jnp.sum(
        jnp.where(hits, requests % sec_local, 0), axis=1
    ).astype(jnp.int32)
    right_t = jnp.transpose(
        right_env.reshape(sec_local, term_local, block_width, 2, half_rows),
        (0, 1, 4, 3, 2),
    ).reshape(sec_local, term_local * half_rows, 2 * block_width)
    send_right = jnp.take(right_t, send_sector, axis=0, mode="clip")
    got_right = lax.all_to_all(send_right, "bond", split_axis=0, concat_axis=0, tiled=True)

    left_flat = left_env.reshape(sec_local, term_local * half_rows, 2 * block_width)
    left_parts = [lax.dynamic_index_in_dim(left_flat, mpo_index, 0, keepdims=False)]
    gain_parts = [gains]
    for shift in range(1, mpo_count):
        target = (mpo_index + shift) % mpo_count
        left_parts.append(
            shifted(lax.dynamic_index_in_dim(left_flat, target, 0, keepdims=False), shift, mpo_count)
        )
        gain_parts.append(shifted(gains, shift, mpo_count))
    left_rows = jnp.stack(left_parts).reshape(
        mpo_count, term_local * block_width, block_width
    )
    gain_rows = jnp.stack(gain_parts).reshape(mpo_count * term_local, class_count)

    mine = lax.dynamic_slice_in_dim(requests, bond_index, 1, axis=0).reshape(
        sec_local, class_count
    )
    sources = (mine // sec_local).astype(jnp.int32)
    targets = (mpo_index + jnp.arange(mpo_count, dtype=jnp.int32)) % mpo_count
    picked = jnp.take(
        got_right, jnp.take(sources, targets, axis=0).reshape(-1), axis=0, mode="clip"
    ).reshape((mpo_count, class_count) + got_right.shape[1:])
    right_rows = [picked[0]] + [
        shifted(picked[shift], shift, mpo_count) for shift in range(1, mpo_count)
    ]

    wave_rows = lax.dynamic_index_in_dim(wave_blocks, mpo_index, 0, keepdims=False)
    done = apply_blocks(gain_rows, wave_rows, left_rows, right_rows)

    out_parts = [done] + [shifted(done, shift, mpo_count) for shift in range(1, mpo_count)]
    full = jnp.zeros((mpo_count,) + done.shape, done.dtype)
    for shift in range(mpo_count):
        owner = (mpo_index - shift) % mpo_count
        full = lax.dynamic_update_index_in_dim(full, out_parts[shift], owner, 0)
    return full


def solution(mesh):
    return jax.shard_map(
        per_device_body,
        mesh=mesh,
        in_specs=(
            P("bond", None, None, None),
            P("bond", "mpo", None),
            P("bond", "mpo", None),
            P("mpo", None),
            P("mpo", None),
            P(),
        ),
        out_specs=P("bond", None, None, None),
        check_vma=False,
    )
```

```python
import jax
import jax.numpy as jnp
from jax import lax
from jax.experimental import pallas as pl
from jax.experimental.pallas import tpu as pltpu
from jax.sharding import PartitionSpec as P


def block_kernel(gain_ref, wave_ref, left_ref, *refs):
    right_refs, out_ref, tiled_ref = refs[:-2], refs[-2], refs[-1]
    block_count, block_width, column_count = wave_ref.shape
    group_count = left_ref.shape[0]
    term_count = gain_ref.shape[0] // group_count
    vectors = column_count // block_width
    lanes = right_refs[0].shape[2]
    half_rows = block_width // 2
    tile_rows = lax.broadcasted_iota(jnp.int32, (lanes, 2 * column_count), 0)
    tile_cols = lax.broadcasted_iota(jnp.int32, (lanes, 2 * column_count), 1)
    lane_tile = (
        (tile_rows // block_width == tile_cols // column_count)
        & (tile_rows % block_width == tile_cols % block_width)
    ).astype(jnp.bfloat16)
    diag_rows = lax.broadcasted_iota(jnp.int32, (column_count, column_count), 0)
    diag_cols = lax.broadcasted_iota(jnp.int32, (column_count, column_count), 1)
    diagonal = diag_rows // block_width == diag_cols // block_width
    half = block_width // 2
    row_in = diag_rows % block_width
    natural = (row_in % half) * 2 + row_in // half
    unpermute = (
        (diag_rows // block_width == diag_cols // block_width)
        & (natural == diag_cols % block_width)
    ).astype(jnp.bfloat16)

    right_rows = right_refs[0].shape[1]
    for g, right_ref in enumerate(right_refs):
        flat = right_ref[...].reshape(block_count * right_rows, lanes)
        tiled_ref[g] = jnp.dot(
            flat, lane_tile, preferred_element_type=jnp.float32
        ).astype(jnp.bfloat16)

    def body(b, carry):
        wave = wave_ref[b]
        total = jnp.zeros((block_width, column_count), jnp.float32)
        for g in range(group_count):
            scaled = []
            for w in range(term_count):
                piece = left_ref[g, w * block_width:(w + 1) * block_width, :]
                gain = gain_ref[g * term_count + w, b]
                scaled.append((piece.astype(jnp.float32) * gain).astype(jnp.bfloat16))
            left_scaled = jnp.concatenate(scaled, axis=0)
            sectioned = jnp.dot(
                left_scaled, wave, preferred_element_type=jnp.float32
            ).astype(jnp.bfloat16)
            tiled = tiled_ref[g, pl.ds(pl.multiple_of(b * right_rows, right_rows), right_rows), :]
            acc = jnp.zeros((block_width, column_count), jnp.float32)
            for w in range(term_count):
                rows_w = tiled[w * half_rows:(w + 1) * half_rows]
                part = jnp.concatenate(
                    [rows_w[:, :column_count], rows_w[:, column_count:]], axis=0
                )
                expanded = jnp.concatenate([part] * vectors, axis=0)
                expanded = jnp.where(diagonal, expanded, jnp.zeros_like(expanded))
                acc = acc + lax.dot_general(
                    sectioned[w * block_width:(w + 1) * block_width],
                    expanded,
                    (((1,), (1,)), ((), ())),
                    preferred_element_type=jnp.float32,
                )
            total = total + acc.astype(jnp.bfloat16).astype(jnp.float32)
        out_ref[b] = jnp.dot(
            total.astype(jnp.bfloat16), unpermute, preferred_element_type=jnp.float32
        ).astype(out_ref.dtype)
        return carry

    lax.fori_loop(0, block_count, body, 0)


def apply_blocks(gains, wave_rows, left_rows, right_rows):
    right_rows = tuple(right_rows)
    block_count, block_width, column_count = wave_rows.shape
    group_count, rows = left_rows.shape[0], left_rows.shape[1]
    flops = block_count * group_count * (
        2 * 2 * rows * block_width * column_count
        + 2 * rows * column_count * column_count
    )
    bytes_accessed = 2 * (
        2 * wave_rows.size + left_rows.size + sum(r.size for r in right_rows)
    )
    vmem = pltpu.MemorySpace.VMEM if hasattr(pltpu, "MemorySpace") else pltpu.VMEM
    return pl.pallas_call(
        block_kernel,
        out_shape=jax.ShapeDtypeStruct(wave_rows.shape, jnp.bfloat16),
        in_specs=[
            pl.BlockSpec(memory_space=pltpu.SMEM),
            pl.BlockSpec(memory_space=vmem),
            pl.BlockSpec(memory_space=vmem),
        ]
        + [pl.BlockSpec(memory_space=vmem)] * len(right_rows),
        out_specs=pl.BlockSpec(memory_space=vmem),
        scratch_shapes=[
            pltpu.VMEM(
                (group_count, block_count * right_rows[0].shape[1], 4 * right_rows[0].shape[2]),
                jnp.bfloat16,
            )
        ],
        cost_estimate=pl.CostEstimate(
            flops=flops, bytes_accessed=bytes_accessed, transcendentals=0
        ),
        compiler_params=pltpu.CompilerParams(

        ),
    )(gains, wave_rows, left_rows, *right_rows)


def shifted(value, shift, count):
    pairs = [(i, (i + shift) % count) for i in range(count)]
    return lax.ppermute(value, "mpo", pairs)


def per_device(wave_blocks, left_env, right_env, mpo_coef, mpo_mask, right_sector):
    sec_local, class_count, block_width, column_count = wave_blocks.shape
    term_local = left_env.shape[1]
    blocks_local = sec_local * class_count
    bond_count = lax.axis_size("bond")
    bond_index = lax.axis_index("bond")
    mpo_count = lax.axis_size("mpo")
    mpo_index = lax.axis_index("mpo")
    half_rows = block_width // 2
    gains = mpo_coef * mpo_mask.astype(jnp.float32)

    requests = right_sector.reshape(bond_count, blocks_local)
    hits = (requests // sec_local) == bond_index
    send_sector = jnp.sum(
        jnp.where(hits, requests % sec_local, 0), axis=1
    ).astype(jnp.int32)
    right_t = right_env.reshape(sec_local, term_local * half_rows, 2 * block_width)
    send_right = jnp.take(right_t, send_sector, axis=0, mode="clip")
    got_right = lax.all_to_all(send_right, "bond", split_axis=0, concat_axis=0, tiled=True)

    left_flat = left_env.reshape(sec_local, term_local * half_rows, 2 * block_width)
    left_parts = [lax.dynamic_index_in_dim(left_flat, mpo_index, 0, keepdims=False)]
    gain_parts = [gains]
    for shift in range(1, mpo_count):
        target = (mpo_index + shift) % mpo_count
        left_parts.append(
            shifted(lax.dynamic_index_in_dim(left_flat, target, 0, keepdims=False), shift, mpo_count)
        )
        gain_parts.append(shifted(gains, shift, mpo_count))
    left_rows = jnp.stack(left_parts).reshape(
        mpo_count, term_local * block_width, block_width
    )
    gain_rows = jnp.stack(gain_parts).reshape(mpo_count * term_local, class_count)

    mine = lax.dynamic_slice_in_dim(requests, bond_index, 1, axis=0).reshape(
        sec_local, class_count
    )
    sources = (mine // sec_local).astype(jnp.int32)
    targets = (mpo_index + jnp.arange(mpo_count, dtype=jnp.int32)) % mpo_count
    picked = jnp.take(
        got_right, jnp.take(sources, targets, axis=0).reshape(-1), axis=0, mode="clip"
    ).reshape((mpo_count, class_count) + got_right.shape[1:])
    right_rows = [picked[0]] + [
        shifted(picked[shift], shift, mpo_count) for shift in range(1, mpo_count)
    ]

    wave_rows = lax.dynamic_index_in_dim(wave_blocks, mpo_index, 0, keepdims=False)
    done = apply_blocks(gain_rows, wave_rows, left_rows, right_rows)

    out_parts = [done] + [shifted(done, shift, mpo_count) for shift in range(1, mpo_count)]
    full = jnp.zeros((mpo_count,) + done.shape, done.dtype)
    for shift in range(mpo_count):
        owner = (mpo_index - shift) % mpo_count
        full = lax.dynamic_update_index_in_dim(full, out_parts[shift], owner, 0)
    return full


def solution(mesh):
    return jax.shard_map(
        per_device,
        mesh=mesh,
        in_specs=(
            P("bond", None, None, None),
            P("bond", "mpo", None),
            P("bond", "mpo", None),
            P("mpo", None),
            P("mpo", None),
            P(),
        ),
        out_specs=P("bond", None, None, None),
        check_vma=False,
    )
```

```python
import jax
import jax.numpy as jnp
from jax import lax
from jax.experimental import pallas as pl
from jax.experimental.pallas import tpu as pltpu
from jax.sharding import PartitionSpec as P


def block_kernel(gain_ref, wave_ref, left_ref, *refs):
    right_refs, out_ref, tiled_ref = refs[:-2], refs[-2], refs[-1]
    block_count, block_width, column_count = wave_ref.shape
    group_count = left_ref.shape[0]
    term_count = gain_ref.shape[0] // group_count
    vectors = column_count // block_width
    lanes = right_refs[0].shape[2]
    half_rows = block_width // 2
    tile_rows = lax.broadcasted_iota(jnp.int32, (lanes, 2 * column_count), 0)
    tile_cols = lax.broadcasted_iota(jnp.int32, (lanes, 2 * column_count), 1)
    lane_tile = (
        (tile_rows // block_width == tile_cols // column_count)
        & (tile_rows % block_width == tile_cols % block_width)
    ).astype(jnp.bfloat16)
    diag_rows = lax.broadcasted_iota(jnp.int32, (column_count, column_count), 0)
    diag_cols = lax.broadcasted_iota(jnp.int32, (column_count, column_count), 1)
    diagonal = diag_rows // block_width == diag_cols // block_width

    right_rows = right_refs[0].shape[1]
    for g, right_ref in enumerate(right_refs):
        flat = right_ref[...].reshape(block_count * right_rows, lanes)
        tiled_ref[g] = jnp.dot(
            flat, lane_tile, preferred_element_type=jnp.float32
        ).astype(jnp.bfloat16)

    def body(b, carry):
        wave = wave_ref[b]
        total = jnp.zeros((block_width, column_count), jnp.float32)
        for g in range(group_count):
            scaled = []
            for w in range(term_count):
                piece = left_ref[g, w * block_width:(w + 1) * block_width, :]
                gain = gain_ref[g * term_count + w, b]
                scaled.append((piece.astype(jnp.float32) * gain).astype(jnp.bfloat16))
            left_scaled = jnp.concatenate(scaled, axis=0)
            sectioned = jnp.dot(
                left_scaled, wave, preferred_element_type=jnp.float32
            ).astype(jnp.bfloat16)
            tiled = tiled_ref[g, pl.ds(pl.multiple_of(b * right_rows, right_rows), right_rows), :]
            acc = jnp.zeros((block_width, column_count), jnp.float32)
            for w in range(term_count):
                rows_w = tiled[w * half_rows:(w + 1) * half_rows]
                part = jnp.concatenate(
                    [rows_w[:, :column_count], rows_w[:, column_count:]], axis=0
                )
                expanded = jnp.concatenate([part] * vectors, axis=0)
                expanded = jnp.where(diagonal, expanded, jnp.zeros_like(expanded))
                acc = acc + jnp.dot(
                    sectioned[w * block_width:(w + 1) * block_width],
                    expanded,
                    preferred_element_type=jnp.float32,
                )
            total = total + acc.astype(jnp.bfloat16).astype(jnp.float32)
        out_ref[b] = total.astype(out_ref.dtype)
        return carry

    lax.fori_loop(0, block_count, body, 0)


def apply_blocks(gains, wave_rows, left_rows, right_rows):
    right_rows = tuple(right_rows)
    block_count, block_width, column_count = wave_rows.shape
    group_count, rows = left_rows.shape[0], left_rows.shape[1]
    flops = block_count * group_count * (
        2 * 2 * rows * block_width * column_count
        + 2 * rows * column_count * column_count
    )
    bytes_accessed = 2 * (
        2 * wave_rows.size + left_rows.size + sum(r.size for r in right_rows)
    )
    vmem = pltpu.MemorySpace.VMEM if hasattr(pltpu, "MemorySpace") else pltpu.VMEM
    return pl.pallas_call(
        block_kernel,
        out_shape=jax.ShapeDtypeStruct(wave_rows.shape, jnp.bfloat16),
        in_specs=[
            pl.BlockSpec(memory_space=pltpu.SMEM),
            pl.BlockSpec(memory_space=vmem),
            pl.BlockSpec(memory_space=vmem),
        ]
        + [pl.BlockSpec(memory_space=vmem)] * len(right_rows),
        out_specs=pl.BlockSpec(memory_space=vmem),
        scratch_shapes=[
            pltpu.VMEM(
                (group_count, block_count * right_rows[0].shape[1], 4 * right_rows[0].shape[2]),
                jnp.bfloat16,
            )
        ],
        cost_estimate=pl.CostEstimate(
            flops=flops, bytes_accessed=bytes_accessed, transcendentals=0
        ),
        compiler_params=pltpu.CompilerParams(

        ),
    )(gains, wave_rows, left_rows, *right_rows)


def shifted(value, shift, count):
    pairs = [(i, (i + shift) % count) for i in range(count)]
    return lax.ppermute(value, "mpo", pairs)


def per_device(wave_blocks, left_env, right_env, mpo_coef, mpo_mask, right_sector):
    sec_local, class_count, block_width, column_count = wave_blocks.shape
    term_local = left_env.shape[1]
    blocks_local = sec_local * class_count
    bond_count = lax.axis_size("bond")
    bond_index = lax.axis_index("bond")
    mpo_count = lax.axis_size("mpo")
    mpo_index = lax.axis_index("mpo")
    half_rows = block_width // 2
    gains = mpo_coef * mpo_mask.astype(jnp.float32)

    requests = right_sector.reshape(bond_count, blocks_local)
    hits = (requests // sec_local) == bond_index
    send_sector = jnp.sum(
        jnp.where(hits, requests % sec_local, 0), axis=1
    ).astype(jnp.int32)
    right_t = jnp.transpose(
        right_env.reshape(sec_local, term_local, block_width, 2, half_rows),
        (0, 1, 4, 3, 2),
    ).reshape(sec_local, term_local * half_rows, 2 * block_width)
    pick = (
        send_sector[:, None] == jnp.arange(sec_local, dtype=jnp.int32)[None, :]
    ).astype(jnp.bfloat16)
    send_right = jnp.dot(
        pick, right_t.reshape(sec_local, -1), preferred_element_type=jnp.float32
    ).astype(jnp.bfloat16).reshape((bond_count,) + right_t.shape[1:])
    got_right = lax.all_to_all(send_right, "bond", split_axis=0, concat_axis=0, tiled=True)

    left_flat = left_env.reshape(sec_local, term_local * half_rows, 2 * block_width)
    left_parts = [lax.dynamic_index_in_dim(left_flat, mpo_index, 0, keepdims=False)]
    gain_parts = [gains]
    for shift in range(1, mpo_count):
        target = (mpo_index + shift) % mpo_count
        left_parts.append(
            shifted(lax.dynamic_index_in_dim(left_flat, target, 0, keepdims=False), shift, mpo_count)
        )
        gain_parts.append(shifted(gains, shift, mpo_count))
    left_rows = jnp.stack(left_parts).reshape(
        mpo_count, term_local * block_width, block_width
    )
    gain_rows = jnp.stack(gain_parts).reshape(mpo_count * term_local, class_count)

    mine = lax.dynamic_slice_in_dim(requests, bond_index, 1, axis=0).reshape(
        sec_local, class_count
    )
    sources = (mine // sec_local).astype(jnp.int32)
    targets = (mpo_index + jnp.arange(mpo_count, dtype=jnp.int32)) % mpo_count
    picked = jnp.take(
        got_right, jnp.take(sources, targets, axis=0).reshape(-1), axis=0, mode="clip"
    ).reshape((mpo_count, class_count) + got_right.shape[1:])
    right_rows = [picked[0]] + [
        shifted(picked[shift], shift, mpo_count) for shift in range(1, mpo_count)
    ]

    wave_rows = lax.dynamic_index_in_dim(wave_blocks, mpo_index, 0, keepdims=False)
    done = apply_blocks(gain_rows, wave_rows, left_rows, right_rows)

    out_parts = [done] + [shifted(done, shift, mpo_count) for shift in range(1, mpo_count)]
    full = jnp.zeros((mpo_count,) + done.shape, done.dtype)
    for shift in range(mpo_count):
        owner = (mpo_index - shift) % mpo_count
        full = lax.dynamic_update_index_in_dim(full, out_parts[shift], owner, 0)
    return full


def solution(mesh):
    return jax.shard_map(
        per_device,
        mesh=mesh,
        in_specs=(
            P("bond", None, None, None),
            P("bond", "mpo", None),
            P("bond", "mpo", None),
            P("mpo", None),
            P("mpo", None),
            P(),
        ),
        out_specs=P("bond", None, None, None),
        check_vma=False,
    )
```

```python
import jax
import jax.numpy as jnp
from jax import lax
from jax.experimental import pallas as pl
from jax.experimental.pallas import tpu as pltpu
from jax.sharding import PartitionSpec as P


def block_kernel(gain_ref, wave_ref, left_ref, *refs):
    right_refs, out_ref, tiled_ref = refs[:-2], refs[-2], refs[-1]
    block_count, block_width, column_count = wave_ref.shape
    group_count = left_ref.shape[0]
    term_count = gain_ref.shape[0] // group_count
    vectors = column_count // block_width
    lanes = right_refs[0].shape[2]
    half_rows = block_width // 2
    tile_rows = lax.broadcasted_iota(jnp.int32, (lanes, 2 * column_count), 0)
    tile_cols = lax.broadcasted_iota(jnp.int32, (lanes, 2 * column_count), 1)
    lane_tile = (
        (tile_rows // block_width == tile_cols // column_count)
        & (tile_rows % block_width == tile_cols % block_width)
    ).astype(jnp.bfloat16)
    diag_rows = lax.broadcasted_iota(jnp.int32, (column_count, column_count), 0)
    diag_cols = lax.broadcasted_iota(jnp.int32, (column_count, column_count), 1)
    diagonal = diag_rows // block_width == diag_cols // block_width

    right_rows = right_refs[0].shape[1]
    for g, right_ref in enumerate(right_refs):
        flat = right_ref[...].reshape(block_count * right_rows, lanes)
        halves = [flat[:, h * block_width:(h + 1) * block_width] for h in range(2)]
        tiled_ref[g] = jnp.concatenate(
            [halves[0]] * vectors + [halves[1]] * vectors, axis=1
        )

    def body(b, carry):
        wave = wave_ref[b]
        total = jnp.zeros((block_width, column_count), jnp.float32)
        for g in range(group_count):
            scaled = []
            for w in range(term_count):
                piece = left_ref[g, w * block_width:(w + 1) * block_width, :]
                gain = gain_ref[g * term_count + w, b]
                scaled.append((piece.astype(jnp.float32) * gain).astype(jnp.bfloat16))
            left_scaled = jnp.concatenate(scaled, axis=0)
            sectioned = jnp.dot(
                left_scaled, wave, preferred_element_type=jnp.float32
            ).astype(jnp.bfloat16)
            tiled = tiled_ref[g, pl.ds(pl.multiple_of(b * right_rows, right_rows), right_rows), :]
            acc = jnp.zeros((block_width, column_count), jnp.float32)
            for w in range(term_count):
                rows_w = tiled[w * half_rows:(w + 1) * half_rows]
                part = jnp.concatenate(
                    [rows_w[:, :column_count], rows_w[:, column_count:]], axis=0
                )
                expanded = jnp.concatenate([part] * vectors, axis=0)
                expanded = jnp.where(diagonal, expanded, jnp.zeros_like(expanded))
                acc = acc + jnp.dot(
                    sectioned[w * block_width:(w + 1) * block_width],
                    expanded,
                    preferred_element_type=jnp.float32,
                )
            total = total + acc.astype(jnp.bfloat16).astype(jnp.float32)
        out_ref[b] = total.astype(out_ref.dtype)
        return carry

    lax.fori_loop(0, block_count, body, 0)


def apply_blocks(gains, wave_rows, left_rows, right_rows):
    right_rows = tuple(right_rows)
    block_count, block_width, column_count = wave_rows.shape
    group_count, rows = left_rows.shape[0], left_rows.shape[1]
    flops = block_count * group_count * (
        2 * 2 * rows * block_width * column_count
        + 2 * rows * column_count * column_count
    )
    bytes_accessed = 2 * (
        2 * wave_rows.size + left_rows.size + sum(r.size for r in right_rows)
    )
    vmem = pltpu.MemorySpace.VMEM if hasattr(pltpu, "MemorySpace") else pltpu.VMEM
    return pl.pallas_call(
        block_kernel,
        out_shape=jax.ShapeDtypeStruct(wave_rows.shape, jnp.bfloat16),
        in_specs=[
            pl.BlockSpec(memory_space=pltpu.SMEM),
            pl.BlockSpec(memory_space=vmem),
            pl.BlockSpec(memory_space=vmem),
        ]
        + [pl.BlockSpec(memory_space=vmem)] * len(right_rows),
        out_specs=pl.BlockSpec(memory_space=vmem),
        scratch_shapes=[
            pltpu.VMEM(
                (group_count, block_count * right_rows[0].shape[1], 4 * right_rows[0].shape[2]),
                jnp.bfloat16,
            )
        ],
        cost_estimate=pl.CostEstimate(
            flops=flops, bytes_accessed=bytes_accessed, transcendentals=0
        ),
        compiler_params=pltpu.CompilerParams(

        ),
    )(gains, wave_rows, left_rows, *right_rows)


def shifted(value, shift, count):
    pairs = [(i, (i + shift) % count) for i in range(count)]
    return lax.ppermute(value, "mpo", pairs)


def per_device(wave_blocks, left_env, right_env, mpo_coef, mpo_mask, right_sector):
    sec_local, class_count, block_width, column_count = wave_blocks.shape
    term_local = left_env.shape[1]
    blocks_local = sec_local * class_count
    bond_count = lax.axis_size("bond")
    bond_index = lax.axis_index("bond")
    mpo_count = lax.axis_size("mpo")
    mpo_index = lax.axis_index("mpo")
    half_rows = block_width // 2
    gains = mpo_coef * mpo_mask.astype(jnp.float32)

    requests = right_sector.reshape(bond_count, blocks_local)
    hits = (requests // sec_local) == bond_index
    send_sector = jnp.sum(
        jnp.where(hits, requests % sec_local, 0), axis=1
    ).astype(jnp.int32)
    right_t = jnp.transpose(
        right_env.reshape(sec_local, term_local, block_width, 2, half_rows),
        (0, 1, 4, 3, 2),
    ).reshape(sec_local, term_local * half_rows, 2 * block_width)
    send_right = jnp.take(right_t, send_sector, axis=0, mode="clip")
    got_right = lax.all_to_all(send_right, "bond", split_axis=0, concat_axis=0, tiled=True)

    left_flat = left_env.reshape(sec_local, term_local * half_rows, 2 * block_width)
    left_parts = [lax.dynamic_index_in_dim(left_flat, mpo_index, 0, keepdims=False)]
    gain_parts = [gains]
    for shift in range(1, mpo_count):
        target = (mpo_index + shift) % mpo_count
        left_parts.append(
            shifted(lax.dynamic_index_in_dim(left_flat, target, 0, keepdims=False), shift, mpo_count)
        )
        gain_parts.append(shifted(gains, shift, mpo_count))
    left_rows = jnp.stack(left_parts).reshape(
        mpo_count, term_local * block_width, block_width
    )
    gain_rows = jnp.stack(gain_parts).reshape(mpo_count * term_local, class_count)

    mine = lax.dynamic_slice_in_dim(requests, bond_index, 1, axis=0).reshape(
        sec_local, class_count
    )
    sources = (mine // sec_local).astype(jnp.int32)
    targets = (mpo_index + jnp.arange(mpo_count, dtype=jnp.int32)) % mpo_count
    picked = jnp.take(
        got_right, jnp.take(sources, targets, axis=0).reshape(-1), axis=0, mode="clip"
    ).reshape((mpo_count, class_count) + got_right.shape[1:])
    right_rows = [picked[0]] + [
        shifted(picked[shift], shift, mpo_count) for shift in range(1, mpo_count)
    ]

    wave_rows = lax.dynamic_index_in_dim(wave_blocks, mpo_index, 0, keepdims=False)
    done = apply_blocks(gain_rows, wave_rows, left_rows, right_rows)

    out_parts = [done] + [shifted(done, shift, mpo_count) for shift in range(1, mpo_count)]
    full = jnp.zeros((mpo_count,) + done.shape, done.dtype)
    for shift in range(mpo_count):
        owner = (mpo_index - shift) % mpo_count
        full = lax.dynamic_update_index_in_dim(full, out_parts[shift], owner, 0)
    return full


def solution(mesh):
    return jax.shard_map(
        per_device,
        mesh=mesh,
        in_specs=(
            P("bond", None, None, None),
            P("bond", "mpo", None),
            P("bond", "mpo", None),
            P("mpo", None),
            P("mpo", None),
            P(),
        ),
        out_specs=P("bond", None, None, None),
        check_vma=False,
    )
```
